512 devices in a mesh: ang: 64 (over x, z_lo, y), rad: 8 (over z_hi, core).
Axes of the slice: x: 4, y: 4, z: 16 (z_hi: 4, z_lo: 4; z = z_hi * 4 + z_lo), core: 2. Of those that a mesh axis runs over, the one named last changes fastest.
Arguments:
- latent: float32 [704, 16384], P('rad', 'ang'), may hold values from -6 to 6
- stencil: float32 [704, 9], P('rad'), may hold values from 0.05 to 0.3
- bin_width: float32 [704], P('rad'), may hold values from 0.0005 to 0.005
- neighbours: int32 [9, 16384], P(None, 'ang'), may hold values from 0 to 511, as said below
- star_bin: int32 [131072], P('ang'), may hold values from 0 to 702
- star_pixels: int32 [4, 131072], P(None, 'ang'), may hold values from 0 to 255
- star_weights: float32 [4, 131072], P(None, 'ang'), may hold values from 0.05 to 1
- star_frac: float32 [131072], P('ang'), may hold values from 0 to 1
- observed: float32 [131072], P('ang'), may hold values from -8 to 8
- sigma: float32 [131072], P('ang'), may hold values from 0.2 to 1
Outputs:
- predicted: float32 [131072], P('ang')
- gradient: float32 [704, 16384], P('rad', 'ang')
The draws below stay inside these ranges and needn't reach their ends.
Inputs may be any that keep to these rules, and one draw needn't show every extreme that they name: For pixel n at cycle r and column c of its patch, neighbours[0, n] = (r + 1) * 128 + c, and every neighbours[k, n] lies in frame cycle r, r + 1 or r + 2.
All inputs are finite; a program needn't handle non-finite values.
Results may differ from the reference program's by a relative error of at most 0.00013.
Values sent between devices are 32-bit elements; how exact they have to be, the bound alone decides.
No kernel may reach another device: no remote copies, remote signals or barrier semaphores. Data moves between devices by JAX's collectives and lax.ppermute only.
A program may use at most 64 MiB of HBM per device.

```python
import math
import jax
import jax.numpy as jnp

BINS = 704
ROWS = 2
COLS = 128
NSTAR_DEV = 2048
PIXELS = 16384
NSTARS = 131072
N_ANG = 64


def draw_neighbours(key, part):
    patch_size = ROWS * COLS
    local = jnp.arange(PIXELS, dtype=jnp.int32) % patch_size
    cycle = local // COLS
    column = local % COLS
    cycle_step = jnp.array([0, -1, -1, -1, 0, 0, 1, 1, 1], jnp.int32)
    column_step = jnp.array([0, -1, 0, 1, -1, 1, -1, 0, 1], jnp.int32)
    jitter = jax.random.randint(key, (9, PIXELS), -1, 2, dtype=jnp.int32)
    jitter = jitter * (cycle_step != 0).astype(jnp.int32)[:, None]
    frame_cycle = cycle[None, :] + 1 + cycle_step[:, None]
    frame_column = (column[None, :] + column_step[:, None] + jitter + COLS) % COLS
    return (frame_cycle * COLS + frame_column).astype(jnp.int32)


def set_ends(values, key, low, top_value):
    place = [jax.random.randint(jax.random.fold_in(key, axis), (), 0, length) for axis, length in enumerate(values.shape)]
    main_axis = values.shape.index(max(values.shape))
    beside = place[:main_axis] + [(place[main_axis] + 1) % values.shape[main_axis]] + place[main_axis + 1:]
    return values.at[tuple(place)].set(low).at[tuple(beside)].set(top_value)


def steps_of(rng, dims, cuts, low, largest):
    def one(position, blocks):
        draws = jax.random.uniform(jax.random.fold_in(jax.random.fold_in(rng, 6), position), (blocks,), jnp.float32, low / len(cuts), largest / len(cuts))
        return jnp.repeat(jnp.exp(draws), dims[position] // blocks).reshape((-1,) + (1,) * (len(dims) - position - 1))

    level = one(*cuts[0])
    for cut in cuts[1:]:
        level = level * one(*cut)
    return level


def noise(own_key, dims, spread, bound, pieces=(), held_as=jnp.bfloat16):
    result = jax.random.normal(own_key, dims, jnp.float32) * spread
    if len(pieces) > 0:
        result = steps_of(own_key, dims, pieces, -0.22, 0.18) * result
    return jnp.clip(result, min=-bound, max=bound).astype(held_as)


def setup_inputs(seed: int = 0) -> dict:
    keys = jax.random.split(jax.random.key(seed), 11)
    return {
        "latent": noise(keys[0], (BINS, PIXELS), 1.0, 6.0, ((0, 8), (1, 64)), jnp.float32),
        "stencil": jnp.clip(0.05 + 0.25 * jax.random.uniform(keys[1], (BINS, 9), jnp.float32) ** steps_of(keys[1], (BINS, 9), ((0, 8),), -0.2, 0.2), 0.05, 0.3),
        "bin_width": jnp.clip(jnp.exp(math.log(0.005) - 2.30258502 * jax.random.uniform(keys[2], (BINS,), jnp.float32) ** steps_of(keys[2], (BINS,), ((0, 8),), -0.2, 0.2)), 0.0005, 0.005),
        "neighbours": draw_neighbours(jax.random.fold_in(keys[10], 71), 0),
        "star_bin": set_ends(jax.random.randint(keys[4], (NSTARS,), 0, BINS - 1), jax.random.fold_in(keys[4], 1), 0, (BINS - 1) - 1).astype(jnp.int32),
        "star_pixels": set_ends(jax.random.randint(keys[5], (4, NSTARS), 0, ROWS * COLS), jax.random.fold_in(keys[5], 1), 0, (ROWS * COLS) - 1).astype(jnp.int32),
        "star_weights": jnp.clip(0.05 + 0.95 * jax.random.uniform(keys[6], (4, NSTARS), jnp.float32) ** steps_of(keys[6], (4, NSTARS), ((1, 64),), -0.2, 0.2), 0.05, 1.0),
        "star_frac": jnp.clip(1.0 * jax.random.uniform(keys[7], (NSTARS,), jnp.float32) ** steps_of(keys[7], (NSTARS,), ((0, 64),), -0.2, 0.2), 0.0, 1.0),
        "observed": noise(keys[8], (NSTARS,), 2.0, 8.0, ((0, 64),), jnp.float32),
        "sigma": jnp.clip(jnp.exp(math.log(1.0) - 1.609438 * jax.random.uniform(keys[9], (NSTARS,), jnp.float32) ** steps_of(keys[9], (NSTARS,), ((0, 64),), -0.2, 0.2)), 0.2, 1.0),
    }


def extend(field):
    shaped = field.reshape(BINS, N_ANG, ROWS, COLS)
    above = jnp.roll(shaped[:, :, ROWS - 1, :], 1, axis=1)
    below = jnp.roll(shaped[:, :, 0, :], -1, axis=1)
    whole = jnp.concatenate([above[:, :, None, :], shaped, below[:, :, None, :]], axis=2)
    return whole.reshape(BINS, N_ANG, (ROWS + 2) * COLS)

def forward(latent, stencil, bin_width, neighbours, star_bin, star_pixels, star_weights, star_frac):
    wide = extend(latent)
    table = neighbours.reshape(9, N_ANG, ROWS * COLS)
    refined = jnp.zeros((BINS, N_ANG, ROWS * COLS), latent.dtype)
    for offset in range(9):
        picks = jnp.broadcast_to(table[offset][None, :, :], (BINS, N_ANG, ROWS * COLS))
        picked = jnp.take_along_axis(wide, picks, axis=2)
        refined = refined + stencil[:, offset][:, None, None] * picked
    density = jnp.exp(refined.reshape(BINS, PIXELS))
    extinction = jnp.cumsum(bin_width[:, None] * density, axis=0)
    patch_start = jnp.arange(NSTARS, dtype=jnp.int32) // NSTAR_DEV * (ROWS * COLS)
    predicted = jnp.zeros((NSTARS,), latent.dtype)
    for corner in range(4):
        pixel = (patch_start + star_pixels[corner]).astype(jnp.int32)
        nearer = extinction[star_bin, pixel]
        farther = extinction[star_bin + 1, pixel]
        predicted = predicted + star_weights[corner] * ((1.0 - star_frac) * nearer + star_frac * farther)
    return predicted

def reference(latent, stencil, bin_width, neighbours, star_bin, star_pixels, star_weights, star_frac, observed, sigma):

    def likelihood(field):
        predicted = forward(field, stencil, bin_width, neighbours, star_bin, star_pixels, star_weights, star_frac)
        scaled = (predicted - observed) / sigma
        return (0.5 * jnp.sum(scaled * scaled), predicted)
    gradient, predicted = jax.grad(likelihood, has_aux=True)(latent)
    return (predicted, gradient)
```

```python
import jax
import jax.numpy as jnp
from jax import lax
from jax.sharding import PartitionSpec as P

COLS = 128
HIGHEST = lax.Precision.HIGHEST


def ring(value, axis, step):
    count = lax.axis_size(axis)
    return lax.ppermute(value, axis, [(i, (i + step) % count) for i in range(count)])


def on_device(
    latent,
    stencil,
    bin_width,
    neighbours,
    star_bin,
    star_pixels,
    star_weights,
    star_frac,
    observed,
    sigma,
):
    shells, pixels = latent.shape
    taps = neighbours.shape[0]
    frame = pixels + 2 * COLS

    above = ring(latent[:, pixels - COLS :], "ang", 1)
    below = ring(latent[:, :COLS], "ang", -1)
    wide = jnp.concatenate([above, latent, below], axis=1)

    position = lax.broadcasted_iota(jnp.int32, (frame, taps * pixels), 0)
    pick = (position == neighbours.reshape(1, taps * pixels)).astype(jnp.float32)
    picked = jnp.dot(wide, pick, precision=HIGHEST, preferred_element_type=jnp.float32)
    refined = jnp.zeros((shells, pixels), jnp.float32)
    for offset in range(taps):
        refined = refined + stencil[:, offset : offset + 1] * picked[:, offset * pixels : (offset + 1) * pixels]
    density = jnp.exp(refined)
    weighted = bin_width[:, None] * density

    nstars = star_bin.shape[0]
    pixel_id = lax.broadcasted_iota(jnp.int32, (pixels, nstars), 0)
    spread = jnp.zeros((pixels, nstars), jnp.float32)
    for corner in range(star_pixels.shape[0]):
        spread = spread + jnp.where(pixel_id == star_pixels[corner][None, :], star_weights[corner][None, :], 0.0)

    shell_start = lax.axis_index("rad") * shells
    bin_id = shell_start + lax.broadcasted_iota(jnp.int32, (shells, nstars), 0)
    lower = star_bin[None, :]
    radial = jnp.where(bin_id <= lower, 1.0, jnp.where(bin_id == lower + 1, star_frac[None, :], 0.0))

    at_stars = jnp.dot(weighted, spread, precision=HIGHEST, preferred_element_type=jnp.float32)
    partial_value = jnp.sum(radial * at_stars, axis=0)
    predicted = lax.psum(partial_value, "rad")
    weight_back = (predicted - observed) / (sigma * sigma)

    adjoint_sum = lax.dot_general(
        radial * weight_back[None, :],
        spread,
        (((1,), (1,)), ((), ())),
        precision=HIGHEST,
        preferred_element_type=jnp.float32,
    )
    sensitivity = adjoint_sum * weighted

    terms = jnp.concatenate(
        [stencil[:, offset : offset + 1] * sensitivity for offset in range(taps)], axis=1
    )
    framed = lax.dot_general(
        terms, pick, (((1,), (1,)), ((), ())), precision=HIGHEST, preferred_element_type=jnp.float32
    )
    from_before = ring(framed[:, frame - COLS :], "ang", 1)
    from_after = ring(framed[:, :COLS], "ang", -1)
    inner = framed[:, COLS : frame - COLS]
    gradient = jnp.concatenate(
        [inner[:, :COLS] + from_before, inner[:, COLS : pixels - COLS], inner[:, pixels - COLS :] + from_after],
        axis=1,
    )
    return (predicted, gradient)


def solution(mesh):
    return jax.shard_map(
        on_device,
        mesh=mesh,
        in_specs=(
            P("rad", "ang"),
            P("rad", None),
            P("rad"),
            P(None, "ang"),
            P("ang"),
            P(None, "ang"),
            P(None, "ang"),
            P("ang"),
            P("ang"),
            P("ang"),
        ),
        out_specs=(P("ang"), P("rad", "ang")),
        check_vma=False,
    )
```

```python
import jax
import jax.numpy as jnp
from jax import lax
from jax.sharding import PartitionSpec as P

COLS = 128
HIGHEST = lax.Precision.HIGHEST


def ring(value, axis, step):
    count = lax.axis_size(axis)
    return lax.ppermute(value, axis, [(i, (i + step) % count) for i in range(count)])


def butterfly_sum(value, axis):
    count = lax.axis_size(axis)
    distance = 1
    while distance < count:
        value = value + lax.ppermute(value, axis, [(i, i ^ distance) for i in range(count)])
        distance *= 2
    return value


def on_device(
    latent,
    stencil,
    bin_width,
    neighbours,
    star_bin,
    star_pixels,
    star_weights,
    star_frac,
    observed,
    sigma,
):
    shells, pixels = latent.shape
    taps = neighbours.shape[0]
    frame = pixels + 2 * COLS

    above = ring(latent[:, pixels - COLS :], "ang", 1)
    below = ring(latent[:, :COLS], "ang", -1)
    wide = jnp.concatenate([above, latent, below], axis=1)

    position = lax.broadcasted_iota(jnp.int32, (frame, taps * pixels), 0)
    pick = (position == neighbours.reshape(1, taps * pixels)).astype(jnp.float32)
    picked = jnp.dot(wide, pick, precision=HIGHEST, preferred_element_type=jnp.float32)
    refined = jnp.zeros((shells, pixels), jnp.float32)
    for offset in range(taps):
        refined = refined + stencil[:, offset : offset + 1] * picked[:, offset * pixels : (offset + 1) * pixels]
    density = jnp.exp(refined)
    weighted = bin_width[:, None] * density

    nstars = star_bin.shape[0]
    pixel_id = lax.broadcasted_iota(jnp.int32, (pixels, nstars), 0)
    spread = jnp.zeros((pixels, nstars), jnp.float32)
    for corner in range(star_pixels.shape[0]):
        spread = spread + jnp.where(pixel_id == star_pixels[corner][None, :], star_weights[corner][None, :], 0.0)

    shell_start = lax.axis_index("rad") * shells
    bin_id = shell_start + lax.broadcasted_iota(jnp.int32, (shells, nstars), 0)
    lower = star_bin[None, :]
    radial = jnp.where(bin_id <= lower, 1.0, jnp.where(bin_id == lower + 1, star_frac[None, :], 0.0))

    at_stars = jnp.dot(weighted, spread, precision=HIGHEST, preferred_element_type=jnp.float32)
    partial_value = jnp.sum(radial * at_stars, axis=0)
    predicted = butterfly_sum(partial_value, "rad")
    weight_back = (predicted - observed) / (sigma * sigma)

    adjoint_sum = lax.dot_general(
        radial * weight_back[None, :],
        spread,
        (((1,), (1,)), ((), ())),
        precision=HIGHEST,
        preferred_element_type=jnp.float32,
    )
    sensitivity = adjoint_sum * weighted

    terms = jnp.concatenate(
        [stencil[:, offset : offset + 1] * sensitivity for offset in range(taps)], axis=1
    )
    framed = lax.dot_general(
        terms, pick, (((1,), (1,)), ((), ())), precision=HIGHEST, preferred_element_type=jnp.float32
    )
    from_before = ring(framed[:, frame - COLS :], "ang", 1)
    from_after = ring(framed[:, :COLS], "ang", -1)
    inner = framed[:, COLS : frame - COLS]
    gradient = jnp.concatenate(
        [inner[:, :COLS] + from_before, inner[:, COLS : pixels - COLS], inner[:, pixels - COLS :] + from_after],
        axis=1,
    )
    return (predicted, gradient)


def solution(mesh):
    return jax.shard_map(
        on_device,
        mesh=mesh,
        in_specs=(
            P("rad", "ang"),
            P("rad", None),
            P("rad"),
            P(None, "ang"),
            P("ang"),
            P(None, "ang"),
            P(None, "ang"),
            P("ang"),
            P("ang"),
            P("ang"),
        ),
        out_specs=(P("ang"), P("rad", "ang")),
        check_vma=False,
    )
```

```python
import jax
import jax.numpy as jnp
from jax import lax
from jax.sharding import PartitionSpec as P

COLS = 128
HIGHEST = lax.Precision.HIGHEST


def ring(value, axis, step):
    count = lax.axis_size(axis)
    return lax.ppermute(value, axis, [(i, (i + step) % count) for i in range(count)])


def on_device(
    latent,
    stencil,
    bin_width,
    neighbours,
    star_bin,
    star_pixels,
    star_weights,
    star_frac,
    observed,
    sigma,
):
    shells, pixels = latent.shape
    taps = neighbours.shape[0]
    frame = pixels + 2 * COLS

    above = ring(latent[:, pixels - COLS :], "ang", 1)
    below = ring(latent[:, :COLS], "ang", -1)
    wide = jnp.concatenate([above, latent, below], axis=1)

    position = lax.broadcasted_iota(jnp.int32, (frame, taps * pixels), 0)
    pick = (position == neighbours.reshape(1, taps * pixels)).astype(jnp.float32)
    picked = jnp.dot(wide, pick, precision=HIGHEST, preferred_element_type=jnp.float32)
    refined = jnp.zeros((shells, pixels), jnp.float32)
    for offset in range(taps):
        refined = refined + stencil[:, offset : offset + 1] * picked[:, offset * pixels : (offset + 1) * pixels]
    density = jnp.exp(refined)
    weighted = bin_width[:, None] * density

    nstars = star_bin.shape[0]
    pixel_id = lax.broadcasted_iota(jnp.int32, (pixels, nstars), 0)
    spread = jnp.zeros((pixels, nstars), jnp.float32)
    for corner in range(star_pixels.shape[0]):
        spread = spread + jnp.where(pixel_id == star_pixels[corner][None, :], star_weights[corner][None, :], 0.0)

    shell_start = lax.axis_index("rad") * shells
    bin_id = shell_start + lax.broadcasted_iota(jnp.int32, (shells, nstars), 0)
    lower = star_bin[None, :]
    radial = jnp.where(bin_id <= lower, 1.0, jnp.where(bin_id == lower + 1, star_frac[None, :], 0.0))

    at_stars = jnp.dot(weighted, spread, precision=HIGHEST, preferred_element_type=jnp.float32)
    partial_value = jnp.sum(radial * at_stars, axis=0)
    predicted = jnp.sum(lax.all_gather(partial_value, "rad"), axis=0)
    weight_back = (predicted - observed) / (sigma * sigma)

    adjoint_sum = lax.dot_general(
        radial * weight_back[None, :],
        spread,
        (((1,), (1,)), ((), ())),
        precision=HIGHEST,
        preferred_element_type=jnp.float32,
    )
    sensitivity = adjoint_sum * weighted

    terms = jnp.concatenate(
        [stencil[:, offset : offset + 1] * sensitivity for offset in range(taps)], axis=1
    )
    framed = lax.dot_general(
        terms, pick, (((1,), (1,)), ((), ())), precision=HIGHEST, preferred_element_type=jnp.float32
    )
    to_after, to_before = lax.optimization_barrier((framed[:, frame - COLS :], framed[:, :COLS]))
    from_before = ring(to_after, "ang", 1)
    from_after = ring(to_before, "ang", -1)
    inner = framed[:, COLS : frame - COLS]
    gradient = jnp.concatenate(
        [inner[:, :COLS] + from_before, inner[:, COLS : pixels - COLS], inner[:, pixels - COLS :] + from_after],
        axis=1,
    )
    return (predicted, gradient)


def solution(mesh):
    return jax.shard_map(
        on_device,
        mesh=mesh,
        in_specs=(
            P("rad", "ang"),
            P("rad", None),
            P("rad"),
            P(None, "ang"),
            P("ang"),
            P(None, "ang"),
            P(None, "ang"),
            P("ang"),
            P("ang"),
            P("ang"),
        ),
        out_specs=(P("ang"), P("rad", "ang")),
        check_vma=False,
    )
```

```python
import jax
import jax.numpy as jnp
from jax import lax
from jax.sharding import PartitionSpec as P

COLS = 128
HIGHEST = lax.Precision.HIGHEST


def ring(value, axis, step):
    count = lax.axis_size(axis)
    return lax.ppermute(value, axis, [(i, (i + step) % count) for i in range(count)])


def on_device(
    latent,
    stencil,
    bin_width,
    neighbours,
    star_bin,
    star_pixels,
    star_weights,
    star_frac,
    observed,
    sigma,
):
    shells, pixels = latent.shape
    taps = neighbours.shape[0]
    frame = pixels + 2 * COLS

    above = ring(latent[:, pixels - COLS :], "ang", 1)
    below = ring(latent[:, :COLS], "ang", -1)
    wide = jnp.concatenate([above, latent, below], axis=1)

    position = lax.broadcasted_iota(jnp.int32, (frame, taps * pixels), 0)
    pick = (position == neighbours.reshape(1, taps * pixels)).astype(jnp.float32)
    picked = jnp.dot(wide, pick, precision=HIGHEST, preferred_element_type=jnp.float32)
    refined = jnp.zeros((shells, pixels), jnp.float32)
    for offset in range(taps):
        refined = refined + stencil[:, offset : offset + 1] * picked[:, offset * pixels : (offset + 1) * pixels]
    density = jnp.exp(refined)
    weighted = bin_width[:, None] * density

    nstars = star_bin.shape[0]
    pixel_id = lax.broadcasted_iota(jnp.int32, (pixels, nstars), 0)
    spread = jnp.zeros((pixels, nstars), jnp.float32)
    for corner in range(star_pixels.shape[0]):
        spread = spread + jnp.where(pixel_id == star_pixels[corner][None, :], star_weights[corner][None, :], 0.0)

    shell_start = lax.axis_index("rad") * shells
    bin_id = shell_start + lax.broadcasted_iota(jnp.int32, (shells, nstars), 0)
    lower = star_bin[None, :]
    radial = jnp.where(bin_id <= lower, 1.0, jnp.where(bin_id == lower + 1, star_frac[None, :], 0.0))

    at_stars = jnp.dot(weighted, spread, precision=HIGHEST, preferred_element_type=jnp.float32)
    partial_value = jnp.sum(radial * at_stars, axis=0)
    count = lax.axis_size("rad")
    copies = jnp.broadcast_to(partial_value[None, :], (count, partial_value.shape[0]))
    predicted = jnp.sum(lax.all_to_all(copies, "rad", 0, 0), axis=0)
    weight_back = (predicted - observed) / (sigma * sigma)

    adjoint_sum = lax.dot_general(
        radial * weight_back[None, :],
        spread,
        (((1,), (1,)), ((), ())),
        precision=HIGHEST,
        preferred_element_type=jnp.float32,
    )
    sensitivity = adjoint_sum * weighted

    terms = jnp.concatenate(
        [stencil[:, offset : offset + 1] * sensitivity for offset in range(taps)], axis=1
    )
    framed = lax.dot_general(
        terms, pick, (((1,), (1,)), ((), ())), precision=HIGHEST, preferred_element_type=jnp.float32
    )
    to_after, to_before = lax.optimization_barrier((framed[:, frame - COLS :], framed[:, :COLS]))
    from_before = ring(to_after, "ang", 1)
    from_after = ring(to_before, "ang", -1)
    inner = framed[:, COLS : frame - COLS]
    gradient = jnp.concatenate(
        [inner[:, :COLS] + from_before, inner[:, COLS : pixels - COLS], inner[:, pixels - COLS :] + from_after],
        axis=1,
    )
    return (predicted, gradient)


def solution(mesh):
    return jax.shard_map(
        on_device,
        mesh=mesh,
        in_specs=(
            P("rad", "ang"),
            P("rad", None),
            P("rad"),
            P(None, "ang"),
            P("ang"),
            P(None, "ang"),
            P(None, "ang"),
            P("ang"),
            P("ang"),
            P("ang"),
        ),
        out_specs=(P("ang"), P("rad", "ang")),
        check_vma=False,
    )
```

```python
import jax
import jax.numpy as jnp
from jax import lax
from jax.sharding import PartitionSpec as P

COLS = 128
HIGHEST = lax.Precision.HIGHEST


def split3(value):
    high = lax.reduce_precision(value, exponent_bits=8, mantissa_bits=7)
    rest = value - high
    middle = lax.reduce_precision(rest, exponent_bits=8, mantissa_bits=7)
    low = rest - middle
    return [part.astype(jnp.bfloat16) for part in (high, middle, low)]


def select(value, onehot):
    total = None
    for part in split3(value):
        product = jnp.dot(part, onehot, preferred_element_type=jnp.float32)
        total = product if total is None else total + product
    return total


def spread_select(value, onehot):
    total = None
    for part in split3(value):
        product = lax.dot_general(part, onehot, (((1,), (1,)), ((), ())), preferred_element_type=jnp.float32)
        total = product if total is None else total + product
    return total


def ring(value, axis, step):
    count = lax.axis_size(axis)
    return lax.ppermute(value, axis, [(i, (i + step) % count) for i in range(count)])


def on_device(
    latent,
    stencil,
    bin_width,
    neighbours,
    star_bin,
    star_pixels,
    star_weights,
    star_frac,
    observed,
    sigma,
):
    shells, pixels = latent.shape
    taps = neighbours.shape[0]
    frame = pixels + 2 * COLS

    above = ring(latent[:, pixels - COLS :], "ang", 1)
    below = ring(latent[:, :COLS], "ang", -1)
    wide = jnp.concatenate([above, latent, below], axis=1)

    cycles = pixels // COLS
    window = 3 * COLS
    rest = taps - 1
    position = lax.broadcasted_iota(jnp.int32, (window, rest * COLS), 0)
    picks = []
    refined_cycles = []
    for cycle in range(cycles):
        columns = neighbours[1:, cycle * COLS : (cycle + 1) * COLS].reshape(1, rest * COLS) - cycle * COLS
        pick = (position == columns).astype(jnp.bfloat16)
        picks.append(pick)
        picked = select(wide[:, cycle * COLS : cycle * COLS + window], pick)
        value = stencil[:, 0:1] * latent[:, cycle * COLS : (cycle + 1) * COLS]
        for offset in range(rest):
            value = value + stencil[:, offset + 1 : offset + 2] * picked[:, offset * COLS : (offset + 1) * COLS]
        refined_cycles.append(value)
    refined = jnp.concatenate(refined_cycles, axis=1)
    density = jnp.exp(refined)
    weighted = bin_width[:, None] * density

    nstars = star_bin.shape[0]
    pixel_id = lax.broadcasted_iota(jnp.int32, (pixels, nstars), 0)
    spread = jnp.zeros((pixels, nstars), jnp.float32)
    for corner in range(star_pixels.shape[0]):
        spread = spread + jnp.where(pixel_id == star_pixels[corner][None, :], star_weights[corner][None, :], 0.0)

    shell_start = lax.axis_index("rad") * shells
    bin_id = shell_start + lax.broadcasted_iota(jnp.int32, (shells, nstars), 0)
    lower = star_bin[None, :]
    radial = jnp.where(bin_id <= lower, 1.0, jnp.where(bin_id == lower + 1, star_frac[None, :], 0.0))

    at_stars = jnp.dot(weighted, spread, precision=HIGHEST, preferred_element_type=jnp.float32)
    partial_value = jnp.sum(radial * at_stars, axis=0)
    predicted = jnp.sum(lax.all_gather(partial_value, "rad"), axis=0)
    weight_back = (predicted - observed) / (sigma * sigma)

    adjoint_sum = lax.dot_general(
        radial * weight_back[None, :],
        spread,
        (((1,), (1,)), ((), ())),
        precision=HIGHEST,
        preferred_element_type=jnp.float32,
    )
    sensitivity = adjoint_sum * weighted

    framed = jnp.pad(stencil[:, 0:1] * sensitivity, ((0, 0), (COLS, COLS)))
    for cycle in range(cycles):
        own = sensitivity[:, cycle * COLS : (cycle + 1) * COLS]
        terms = jnp.concatenate([stencil[:, offset + 1 : offset + 2] * own for offset in range(rest)], axis=1)
        spread_back = spread_select(terms, picks[cycle])
        framed = framed + jnp.pad(spread_back, ((0, 0), (cycle * COLS, frame - window - cycle * COLS)))
    to_after, to_before = lax.optimization_barrier((framed[:, frame - COLS :], framed[:, :COLS]))
    from_before = ring(to_after, "ang", 1)
    from_after = ring(to_before, "ang", -1)
    inner = framed[:, COLS : frame - COLS]
    gradient = jnp.concatenate(
        [inner[:, :COLS] + from_before, inner[:, COLS : pixels - COLS], inner[:, pixels - COLS :] + from_after],
        axis=1,
    )
    return (predicted, gradient)


def solution(mesh):
    return jax.shard_map(
        on_device,
        mesh=mesh,
        in_specs=(
            P("rad", "ang"),
            P("rad", None),
            P("rad"),
            P(None, "ang"),
            P("ang"),
            P(None, "ang"),
            P(None, "ang"),
            P("ang"),
            P("ang"),
            P("ang"),
        ),
        out_specs=(P("ang"), P("rad", "ang")),
        check_vma=False,
    )
```

```python
import jax
import jax.numpy as jnp
from jax import lax
from jax.sharding import PartitionSpec as P

COLS = 128
HIGHEST = lax.Precision.HIGHEST


def split3(value):
    high = lax.reduce_precision(value, exponent_bits=8, mantissa_bits=7)
    rest = value - high
    middle = lax.reduce_precision(rest, exponent_bits=8, mantissa_bits=7)
    low = rest - middle
    return jnp.concatenate([high, middle, low], axis=0).astype(jnp.bfloat16)


def select(value, onehot):
    rows = value.shape[0]
    product = jnp.dot(split3(value), onehot, preferred_element_type=jnp.float32)
    return product[:rows] + product[rows : 2 * rows] + product[2 * rows :]


def spread_select(value, onehot):
    rows = value.shape[0]
    product = lax.dot_general(split3(value), onehot, (((1,), (1,)), ((), ())), preferred_element_type=jnp.float32)
    return product[:rows] + product[rows : 2 * rows] + product[2 * rows :]


def ring(value, axis, step):
    count = lax.axis_size(axis)
    return lax.ppermute(value, axis, [(i, (i + step) % count) for i in range(count)])


def on_device(
    latent,
    stencil,
    bin_width,
    neighbours,
    star_bin,
    star_pixels,
    star_weights,
    star_frac,
    observed,
    sigma,
):
    shells, pixels = latent.shape
    taps = neighbours.shape[0]
    frame = pixels + 2 * COLS

    above = ring(latent[:, pixels - COLS :], "ang", 1)
    below = ring(latent[:, :COLS], "ang", -1)
    wide = jnp.concatenate([above, latent, below], axis=1)

    rest = taps - 1
    position = lax.broadcasted_iota(jnp.int32, (frame, rest * pixels), 0)
    pick = (position == neighbours[1:].reshape(1, rest * pixels)).astype(jnp.bfloat16)
    picked = select(wide, pick)
    refined = stencil[:, 0:1] * latent
    for offset in range(rest):
        refined = refined + stencil[:, offset + 1 : offset + 2] * picked[:, offset * pixels : (offset + 1) * pixels]
    density = jnp.exp(refined)
    weighted = bin_width[:, None] * density

    nstars = star_bin.shape[0]
    pixel_id = lax.broadcasted_iota(jnp.int32, (pixels, nstars), 0)
    spread = jnp.zeros((pixels, nstars), jnp.float32)
    for corner in range(star_pixels.shape[0]):
        spread = spread + jnp.where(pixel_id == star_pixels[corner][None, :], star_weights[corner][None, :], 0.0)

    shell_start = lax.axis_index("rad") * shells
    bin_id = shell_start + lax.broadcasted_iota(jnp.int32, (shells, nstars), 0)
    lower = star_bin[None, :]
    radial = jnp.where(bin_id <= lower, 1.0, jnp.where(bin_id == lower + 1, star_frac[None, :], 0.0))

    at_stars = jnp.dot(weighted, spread, precision=HIGHEST, preferred_element_type=jnp.float32)
    partial_value = jnp.sum(radial * at_stars, axis=0)
    predicted = jnp.sum(lax.all_gather(partial_value, "rad"), axis=0)
    weight_back = (predicted - observed) / (sigma * sigma)

    adjoint_sum = lax.dot_general(
        radial * weight_back[None, :],
        spread,
        (((1,), (1,)), ((), ())),
        precision=HIGHEST,
        preferred_element_type=jnp.float32,
    )
    sensitivity = adjoint_sum * weighted

    terms = jnp.concatenate(
        [stencil[:, offset + 1 : offset + 2] * sensitivity for offset in range(rest)], axis=1
    )
    framed = spread_select(terms, pick) + jnp.pad(stencil[:, 0:1] * sensitivity, ((0, 0), (COLS, COLS)))
    to_after, to_before = lax.optimization_barrier((framed[:, frame - COLS :], framed[:, :COLS]))
    from_before = ring(to_after, "ang", 1)
    from_after = ring(to_before, "ang", -1)
    inner = framed[:, COLS : frame - COLS]
    gradient = jnp.concatenate(
        [inner[:, :COLS] + from_before, inner[:, COLS : pixels - COLS], inner[:, pixels - COLS :] + from_after],
        axis=1,
    )
    return (predicted, gradient)


def solution(mesh):
    return jax.shard_map(
        on_device,
        mesh=mesh,
        in_specs=(
            P("rad", "ang"),
            P("rad", None),
            P("rad"),
            P(None, "ang"),
            P("ang"),
            P(None, "ang"),
            P(None, "ang"),
            P("ang"),
            P("ang"),
            P("ang"),
        ),
        out_specs=(P("ang"), P("rad", "ang")),
        check_vma=False,
    )
```

```python
import jax
import jax.numpy as jnp
from jax import lax
from jax.sharding import PartitionSpec as P

COLS = 128
HIGHEST = lax.Precision.HIGHEST


def split3(value):
    high = lax.reduce_precision(value, exponent_bits=8, mantissa_bits=7)
    rest = value - high
    middle = lax.reduce_precision(rest, exponent_bits=8, mantissa_bits=7)
    low = rest - middle
    return jnp.concatenate([high, middle, low], axis=0).astype(jnp.bfloat16)


def select(value, onehot):
    rows = value.shape[0]
    product = jnp.dot(split3(value), onehot, preferred_element_type=jnp.float32)
    return product[:rows] + product[rows : 2 * rows] + product[2 * rows :]


def spread_select(value, onehot):
    rows = value.shape[0]
    product = lax.dot_general(split3(value), onehot, (((1,), (1,)), ((), ())), preferred_element_type=jnp.float32)
    return product[:rows] + product[rows : 2 * rows] + product[2 * rows :]


def ring(value, axis, step):
    count = lax.axis_size(axis)
    return lax.ppermute(value, axis, [(i, (i + step) % count) for i in range(count)])


def on_device(
    latent,
    stencil,
    bin_width,
    neighbours,
    star_bin,
    star_pixels,
    star_weights,
    star_frac,
    observed,
    sigma,
):
    shells, pixels = latent.shape
    taps = neighbours.shape[0]
    frame = pixels + 2 * COLS

    above = ring(latent[:, pixels - COLS :], "ang", 1)
    below = ring(latent[:, :COLS], "ang", -1)
    wide = jnp.concatenate([above, latent, below], axis=1)

    rest = taps - 1
    position = lax.broadcasted_iota(jnp.int32, (frame, rest * pixels), 0)
    pick = (position == neighbours[1:].reshape(1, rest * pixels)).astype(jnp.bfloat16)
    picked = select(wide, pick)
    scaled = picked.reshape(shells, rest, pixels) * stencil[:, 1:, None]
    refined = stencil[:, 0:1] * latent + jnp.sum(scaled, axis=1)
    density = jnp.exp(refined)
    weighted = bin_width[:, None] * density

    nstars = star_bin.shape[0]
    pixel_id = lax.broadcasted_iota(jnp.int32, (pixels, nstars), 0)
    spread = jnp.sum(jnp.where(pixel_id[None] == star_pixels[:, None, :], star_weights[:, None, :], 0.0), axis=0)

    shell_start = lax.axis_index("rad") * shells
    bin_id = shell_start + lax.broadcasted_iota(jnp.int32, (shells, nstars), 0)
    lower = star_bin[None, :]
    radial = jnp.where(bin_id <= lower, 1.0, jnp.where(bin_id == lower + 1, star_frac[None, :], 0.0))

    at_stars = jnp.dot(weighted, spread, precision=HIGHEST, preferred_element_type=jnp.float32)
    partial_value = jnp.sum(radial * at_stars, axis=0)
    predicted = jnp.sum(lax.all_gather(partial_value, "rad"), axis=0)
    weight_back = (predicted - observed) / (sigma * sigma)

    adjoint_sum = lax.dot_general(
        radial * weight_back[None, :],
        spread,
        (((1,), (1,)), ((), ())),
        precision=HIGHEST,
        preferred_element_type=jnp.float32,
    )
    sensitivity = adjoint_sum * weighted

    terms = (stencil[:, 1:, None] * sensitivity[:, None, :]).reshape(shells, rest * pixels)
    framed = spread_select(terms, pick) + jnp.pad(stencil[:, 0:1] * sensitivity, ((0, 0), (COLS, COLS)))
    to_after, to_before = lax.optimization_barrier((framed[:, frame - COLS :], framed[:, :COLS]))
    from_before = ring(to_after, "ang", 1)
    from_after = ring(to_before, "ang", -1)
    inner = framed[:, COLS : frame - COLS]
    gradient = jnp.concatenate(
        [inner[:, :COLS] + from_before, inner[:, COLS : pixels - COLS], inner[:, pixels - COLS :] + from_after],
        axis=1,
    )
    return (predicted, gradient)


def solution(mesh):
    return jax.shard_map(
        on_device,
        mesh=mesh,
        in_specs=(
            P("rad", "ang"),
            P("rad", None),
            P("rad"),
            P(None, "ang"),
            P("ang"),
            P(None, "ang"),
            P(None, "ang"),
            P("ang"),
            P("ang"),
            P("ang"),
        ),
        out_specs=(P("ang"), P("rad", "ang")),
        check_vma=False,
    )
```

```python
import jax
import jax.numpy as jnp
from jax import lax
from jax.sharding import PartitionSpec as P

COLS = 128
HIGHEST = lax.Precision.HIGHEST


def split3(value):
    high = lax.reduce_precision(value, exponent_bits=8, mantissa_bits=7)
    rest = value - high
    middle = lax.reduce_precision(rest, exponent_bits=8, mantissa_bits=7)
    low = rest - middle
    return jnp.concatenate([high, middle, low], axis=0).astype(jnp.bfloat16)


def select(value, onehot):
    rows = value.shape[0]
    product = lax.dot_general(split3(value), onehot, (((1,), (0,)), ((), ())), preferred_element_type=jnp.float32)
    return product[:rows] + product[rows : 2 * rows] + product[2 * rows :]


def spread_select(value, onehot):
    rows = value.shape[0]
    product = lax.dot_general(
        split3(value), onehot, (((1, 2), (1, 2)), ((), ())), preferred_element_type=jnp.float32
    )
    return product[:rows] + product[rows : 2 * rows] + product[2 * rows :]


def ring(value, axis, step):
    count = lax.axis_size(axis)
    return lax.ppermute(value, axis, [(i, (i + step) % count) for i in range(count)])


def on_device(
    latent,
    stencil,
    bin_width,
    neighbours,
    star_bin,
    star_pixels,
    star_weights,
    star_frac,
    observed,
    sigma,
):
    shells, pixels = latent.shape
    taps = neighbours.shape[0]
    frame = pixels + 2 * COLS

    above = ring(latent[:, pixels - COLS :], "ang", 1)
    below = ring(latent[:, :COLS], "ang", -1)
    wide = jnp.concatenate([above, latent, below], axis=1)

    position = lax.broadcasted_iota(jnp.int32, (frame, taps, pixels), 0)
    pick = (position == neighbours[None, :, :]).astype(jnp.bfloat16)
    picked = select(wide, pick)
    refined = jnp.sum(picked * stencil[:, :, None], axis=1)
    density = jnp.exp(refined)
    weighted = bin_width[:, None] * density

    nstars = star_bin.shape[0]
    pixel_id = lax.broadcasted_iota(jnp.int32, (pixels, nstars), 0)
    spread = jnp.sum(jnp.where(pixel_id[None] == star_pixels[:, None, :], star_weights[:, None, :], 0.0), axis=0)

    shell_start = lax.axis_index("rad") * shells
    bin_id = shell_start + lax.broadcasted_iota(jnp.int32, (shells, nstars), 0)
    lower = star_bin[None, :]
    radial = jnp.where(bin_id <= lower, 1.0, jnp.where(bin_id - 1 == lower, star_frac[None, :], 0.0))

    at_stars = jnp.dot(weighted, spread, precision=HIGHEST, preferred_element_type=jnp.float32)
    partial_value = jnp.sum(radial * at_stars, axis=0)
    predicted = jnp.sum(lax.all_gather(partial_value, "rad"), axis=0)
    weight_back = (predicted - observed) / (sigma * sigma)

    adjoint_sum = lax.dot_general(
        radial * weight_back[None, :],
        spread,
        (((1,), (1,)), ((), ())),
        precision=HIGHEST,
        preferred_element_type=jnp.float32,
    )
    sensitivity = adjoint_sum * weighted

    terms = stencil[:, :, None] * sensitivity[:, None, :]
    framed = spread_select(terms, pick)
    to_after, to_before = lax.optimization_barrier((framed[:, frame - COLS :], framed[:, :COLS]))
    from_before = ring(to_after, "ang", 1)
    from_after = ring(to_before, "ang", -1)
    inner = framed[:, COLS : frame - COLS]
    gradient = jnp.concatenate(
        [inner[:, :COLS] + from_before, inner[:, COLS : pixels - COLS], inner[:, pixels - COLS :] + from_after],
        axis=1,
    )
    return (predicted, gradient)


def solution(mesh):
    return jax.shard_map(
        on_device,
        mesh=mesh,
        in_specs=(
            P("rad", "ang"),
            P("rad", None),
            P("rad"),
            P(None, "ang"),
            P("ang"),
            P(None, "ang"),
            P(None, "ang"),
            P("ang"),
            P("ang"),
            P("ang"),
        ),
        out_specs=(P("ang"), P("rad", "ang")),
        check_vma=False,
    )
```

```python
import jax
import jax.numpy as jnp
from jax import lax
from jax.sharding import PartitionSpec as P

COLS = 128
HIGHEST = lax.Precision.HIGHEST


def split3(value):
    high = lax.reduce_precision(value, exponent_bits=8, mantissa_bits=7)
    rest = value - high
    middle = lax.reduce_precision(rest, exponent_bits=8, mantissa_bits=7)
    low = rest - middle
    return jnp.concatenate([high, middle, low], axis=0).astype(jnp.bfloat16)


def select(value, onehot):
    rows = value.shape[0]
    product = lax.dot_general(split3(value), onehot, (((1,), (0,)), ((), ())), preferred_element_type=jnp.float32)
    return product[:rows] + product[rows : 2 * rows] + product[2 * rows :]


def spread_select(value, onehot):
    rows = value.shape[0]
    product = lax.dot_general(
        split3(value), onehot, (((1, 2), (1, 2)), ((), ())), preferred_element_type=jnp.float32
    )
    return product[:rows] + product[rows : 2 * rows] + product[2 * rows :]


def ring(value, axis, step):
    count = lax.axis_size(axis)
    return lax.ppermute(value, axis, [(i, (i + step) % count) for i in range(count)])


def on_device(
    latent,
    stencil,
    bin_width,
    neighbours,
    star_bin,
    star_pixels,
    star_weights,
    star_frac,
    observed,
    sigma,
):
    shells, pixels = latent.shape
    taps = neighbours.shape[0]
    frame = pixels + 2 * COLS

    above = ring(latent[:, pixels - COLS :], "ang", 1)
    below = ring(latent[:, :COLS], "ang", -1)
    wide = jnp.concatenate([above, latent, below], axis=1)

    position = lax.broadcasted_iota(jnp.int32, (frame, taps, pixels), 0)
    pick = (position == neighbours[None, :, :]).astype(jnp.bfloat16)
    picked = select(wide, pick)
    refined = jnp.sum(picked * stencil[:, :, None], axis=1)
    density = jnp.exp(refined)
    weighted = bin_width[:, None] * density

    nstars = star_bin.shape[0]
    pixel_id = lax.broadcasted_iota(jnp.int32, (pixels, nstars), 0)
    spread = jnp.sum(jnp.where(pixel_id[None] == star_pixels[:, None, :], star_weights[:, None, :], 0.0), axis=0)

    shell_start = lax.axis_index("rad") * shells
    bin_id = shell_start + lax.broadcasted_iota(jnp.int32, (shells, nstars), 0)
    lower = star_bin[None, :]
    radial = jnp.where(bin_id <= lower, 1.0, jnp.where(bin_id - 1 == lower, star_frac[None, :], 0.0))

    at_stars = jnp.dot(weighted, spread, precision=HIGHEST, preferred_element_type=jnp.float32)
    partial_value = jnp.sum(radial * at_stars, axis=0)
    padded = jnp.pad(partial_value, (0, 7 * nstars))
    predicted = lax.psum(padded, "rad")[:nstars]
    weight_back = (predicted - observed) / (sigma * sigma)

    adjoint_sum = lax.dot_general(
        radial * weight_back[None, :],
        spread,
        (((1,), (1,)), ((), ())),
        precision=HIGHEST,
        preferred_element_type=jnp.float32,
    )
    sensitivity = adjoint_sum * weighted

    terms = stencil[:, :, None] * sensitivity[:, None, :]
    framed = spread_select(terms, pick)
    to_after, to_before = lax.optimization_barrier((framed[:, frame - COLS :], framed[:, :COLS]))
    from_before = ring(to_after, "ang", 1)
    from_after = ring(to_before, "ang", -1)
    inner = framed[:, COLS : frame - COLS]
    gradient = jnp.concatenate(
        [inner[:, :COLS] + from_before, inner[:, COLS : pixels - COLS], inner[:, pixels - COLS :] + from_after],
        axis=1,
    )
    return (predicted, gradient)


def solution(mesh):
    return jax.shard_map(
        on_device,
        mesh=mesh,
        in_specs=(
            P("rad", "ang"),
            P("rad", None),
            P("rad"),
            P(None, "ang"),
            P("ang"),
            P(None, "ang"),
            P(None, "ang"),
            P("ang"),
            P("ang"),
            P("ang"),
        ),
        out_specs=(P("ang"), P("rad", "ang")),
        check_vma=False,
    )
```

```python
import jax
import jax.numpy as jnp
from jax import lax
from jax.sharding import Mesh, PartitionSpec as P

COLS = 128
HIGHEST = lax.Precision.HIGHEST


def split3(value):
    high = lax.reduce_precision(value, exponent_bits=8, mantissa_bits=7)
    rest = value - high
    middle = lax.reduce_precision(rest, exponent_bits=8, mantissa_bits=7)
    low = rest - middle
    return jnp.concatenate([high, middle, low], axis=0).astype(jnp.bfloat16)


def select(value, onehot):
    rows = value.shape[0]
    product = lax.dot_general(split3(value), onehot, (((1,), (0,)), ((), ())), preferred_element_type=jnp.float32)
    return product[:rows] + product[rows : 2 * rows] + product[2 * rows :]


def spread_select(value, onehot):
    rows = value.shape[0]
    product = lax.dot_general(
        split3(value), onehot, (((1, 2), (1, 2)), ((), ())), preferred_element_type=jnp.float32
    )
    return product[:rows] + product[rows : 2 * rows] + product[2 * rows :]


def ring(value, axis, step):
    count = lax.axis_size(axis)
    return lax.ppermute(value, axis, [(i, (i + step) % count) for i in range(count)])


def on_device(
    latent,
    stencil,
    bin_width,
    neighbours,
    star_bin,
    star_pixels,
    star_weights,
    star_frac,
    observed,
    sigma,
):
    shells, pixels = latent.shape
    taps = neighbours.shape[0]
    frame = pixels + 2 * COLS

    above = ring(latent[:, pixels - COLS :], "ang", 1)
    below = ring(latent[:, :COLS], "ang", -1)
    wide = jnp.concatenate([above, latent, below], axis=1)

    position = lax.broadcasted_iota(jnp.int32, (frame, taps, pixels), 0)
    pick = (position == neighbours[None, :, :]).astype(jnp.bfloat16)
    picked = select(wide, pick)
    refined = jnp.sum(picked * stencil[:, :, None], axis=1)
    density = jnp.exp(refined)
    weighted = bin_width[:, None] * density

    nstars = star_bin.shape[0]
    pixel_id = lax.broadcasted_iota(jnp.int32, (pixels, nstars), 0)
    spread = jnp.sum(jnp.where(pixel_id[None] == star_pixels[:, None, :], star_weights[:, None, :], 0.0), axis=0)

    shell_start = (lax.axis_index("zhi") * lax.axis_size("core") + lax.axis_index("core")) * shells
    bin_id = shell_start + lax.broadcasted_iota(jnp.int32, (shells, nstars), 0)
    lower = star_bin[None, :]
    radial = jnp.where(bin_id <= lower, 1.0, jnp.where(bin_id - 1 == lower, star_frac[None, :], 0.0))

    at_stars = jnp.dot(weighted, spread, precision=HIGHEST, preferred_element_type=jnp.float32)
    partial_value = jnp.sum(radial * at_stars, axis=0)
    pair = partial_value + lax.ppermute(partial_value, "core", [(0, 1), (1, 0)])
    predicted = jnp.sum(lax.all_gather(pair, "zhi"), axis=0)
    weight_back = (predicted - observed) / (sigma * sigma)

    adjoint_sum = lax.dot_general(
        radial * weight_back[None, :],
        spread,
        (((1,), (1,)), ((), ())),
        precision=HIGHEST,
        preferred_element_type=jnp.float32,
    )
    sensitivity = adjoint_sum * weighted

    terms = stencil[:, :, None] * sensitivity[:, None, :]
    framed = spread_select(terms, pick)
    to_after, to_before = lax.optimization_barrier((framed[:, frame - COLS :], framed[:, :COLS]))
    from_before = ring(to_after, "ang", 1)
    from_after = ring(to_before, "ang", -1)
    inner = framed[:, COLS : frame - COLS]
    gradient = jnp.concatenate(
        [inner[:, :COLS] + from_before, inner[:, COLS : pixels - COLS], inner[:, pixels - COLS :] + from_after],
        axis=1,
    )
    return (predicted, gradient)


def solution(mesh):
    ang, rad = mesh.devices.shape
    split = Mesh(mesh.devices.reshape(ang, rad // 2, 2), ("ang", "zhi", "core"))
    shell = ("zhi", "core")
    return jax.shard_map(
        on_device,
        mesh=split,
        in_specs=(
            P(shell, "ang"),
            P(shell, None),
            P(shell),
            P(None, "ang"),
            P("ang"),
            P(None, "ang"),
            P(None, "ang"),
            P("ang"),
            P("ang"),
            P("ang"),
        ),
        out_specs=(P("ang"), P(shell, "ang")),
        check_vma=False,
    )
```

```python
import jax
import jax.numpy as jnp
from jax import lax
from jax.sharding import PartitionSpec as P

COLS = 128
HIGHEST = lax.Precision.HIGHEST


def split3(value):
    high = lax.reduce_precision(value, exponent_bits=8, mantissa_bits=7)
    rest = value - high
    middle = lax.reduce_precision(rest, exponent_bits=8, mantissa_bits=7)
    low = rest - middle
    return jnp.concatenate([high, middle, low], axis=0).astype(jnp.bfloat16)


def select(value, onehot):
    rows = value.shape[0]
    product = lax.dot_general(split3(value), onehot, (((1,), (0,)), ((), ())), preferred_element_type=jnp.float32)
    return product[:rows] + product[rows : 2 * rows] + product[2 * rows :]


def spread_select(value, onehot):
    rows = value.shape[0]
    product = lax.dot_general(
        split3(value), onehot, (((1, 2), (1, 2)), ((), ())), preferred_element_type=jnp.float32
    )
    return product[:rows] + product[rows : 2 * rows] + product[2 * rows :]


def ring(value, axis, step):
    count = lax.axis_size(axis)
    return lax.ppermute(value, axis, [(i, (i + step) % count) for i in range(count)])


def on_device(
    latent,
    stencil,
    bin_width,
    neighbours,
    star_bin,
    star_pixels,
    star_weights,
    star_frac,
    observed,
    sigma,
):
    shells, pixels = latent.shape
    taps = neighbours.shape[0]
    frame = pixels + 2 * COLS

    before = ring(latent, "ang", 1)
    after = ring(latent, "ang", -1)
    wide = jnp.concatenate([before[:, pixels - COLS :], latent, after[:, :COLS]], axis=1)

    position = lax.broadcasted_iota(jnp.int32, (frame, taps, pixels), 0)
    pick = (position == neighbours[None, :, :]).astype(jnp.bfloat16)
    picked = select(wide, pick)
    refined = jnp.sum(picked * stencil[:, :, None], axis=1)
    density = jnp.exp(refined)
    weighted = bin_width[:, None] * density

    nstars = star_bin.shape[0]
    pixel_id = lax.broadcasted_iota(jnp.int32, (pixels, nstars), 0)
    spread = jnp.sum(jnp.where(pixel_id[None] == star_pixels[:, None, :], star_weights[:, None, :], 0.0), axis=0)

    shell_start = lax.axis_index("rad") * shells
    bin_id = shell_start + lax.broadcasted_iota(jnp.int32, (shells, nstars), 0)
    lower = star_bin[None, :]
    radial = jnp.where(bin_id <= lower, 1.0, jnp.where(bin_id - 1 == lower, star_frac[None, :], 0.0))

    at_stars = jnp.dot(weighted, spread, precision=HIGHEST, preferred_element_type=jnp.float32)
    partial_value = jnp.sum(radial * at_stars, axis=0)
    predicted = jnp.sum(lax.all_gather(partial_value, "rad"), axis=0)
    weight_back = (predicted - observed) / (sigma * sigma)

    adjoint_sum = lax.dot_general(
        radial * weight_back[None, :],
        spread,
        (((1,), (1,)), ((), ())),
        precision=HIGHEST,
        preferred_element_type=jnp.float32,
    )
    sensitivity = adjoint_sum * weighted

    terms = stencil[:, :, None] * sensitivity[:, None, :]
    framed = spread_select(terms, pick)
    to_after, to_before = lax.optimization_barrier((framed[:, frame - COLS :], framed[:, :COLS]))
    from_before = ring(to_after, "ang", 1)
    from_after = ring(to_before, "ang", -1)
    inner = framed[:, COLS : frame - COLS]
    gradient = jnp.concatenate(
        [inner[:, :COLS] + from_before, inner[:, COLS : pixels - COLS], inner[:, pixels - COLS :] + from_after],
        axis=1,
    )
    return (predicted, gradient)


def solution(mesh):
    return jax.shard_map(
        on_device,
        mesh=mesh,
        in_specs=(
            P("rad", "ang"),
            P("rad", None),
            P("rad"),
            P(None, "ang"),
            P("ang"),
            P(None, "ang"),
            P(None, "ang"),
            P("ang"),
            P("ang"),
            P("ang"),
        ),
        out_specs=(P("ang"), P("rad", "ang")),
        check_vma=False,
    )
```

```python
import jax
import jax.numpy as jnp
from jax import lax
from jax.sharding import Mesh, PartitionSpec as P

COLS = 128
HIGHEST = lax.Precision.HIGHEST


def split3(value):
    high = lax.reduce_precision(value, exponent_bits=8, mantissa_bits=7)
    rest = value - high
    middle = lax.reduce_precision(rest, exponent_bits=8, mantissa_bits=7)
    low = rest - middle
    return jnp.concatenate([high, middle, low], axis=0).astype(jnp.bfloat16)


def select(value, onehot):
    rows = value.shape[0]
    product = lax.dot_general(split3(value), onehot, (((1,), (0,)), ((), ())), preferred_element_type=jnp.float32)
    return product[:rows] + product[rows : 2 * rows] + product[2 * rows :]


def spread_select(value, onehot):
    rows = value.shape[0]
    product = lax.dot_general(
        split3(value), onehot, (((1, 2), (1, 2)), ((), ())), preferred_element_type=jnp.float32
    )
    return product[:rows] + product[rows : 2 * rows] + product[2 * rows :]


def ring(value, axis, step):
    count = lax.axis_size(axis)
    return lax.ppermute(value, axis, [(i, (i + step) % count) for i in range(count)])


def on_device(
    latent,
    stencil,
    bin_width,
    neighbours,
    star_bin,
    star_pixels,
    star_weights,
    star_frac,
    observed,
    sigma,
):
    shells, pixels = latent.shape
    taps = neighbours.shape[0]
    frame = pixels + 2 * COLS

    before = ring(latent, "ang", 1)
    after = ring(latent, "ang", -1)
    wide = jnp.concatenate([before[:, pixels - COLS :], latent, after[:, :COLS]], axis=1)

    position = lax.broadcasted_iota(jnp.int32, (frame, taps, pixels), 0)
    pick = (position == neighbours[None, :, :]).astype(jnp.bfloat16)
    picked = select(wide, pick)
    refined = jnp.sum(picked * stencil[:, :, None], axis=1)
    density = jnp.exp(refined)
    weighted = bin_width[:, None] * density

    nstars = star_bin.shape[0]
    pixel_id = lax.broadcasted_iota(jnp.int32, (pixels, nstars), 0)
    spread = jnp.sum(jnp.where(pixel_id[None] == star_pixels[:, None, :], star_weights[:, None, :], 0.0), axis=0)

    shell_start = (lax.axis_index("zhi") * lax.axis_size("core") + lax.axis_index("core")) * shells
    bin_id = shell_start + lax.broadcasted_iota(jnp.int32, (shells, nstars), 0)
    lower = star_bin[None, :]
    radial = jnp.where(bin_id <= lower, 1.0, jnp.where(bin_id - 1 == lower, star_frac[None, :], 0.0))

    at_stars = jnp.dot(weighted, spread, precision=HIGHEST, preferred_element_type=jnp.float32)
    partial_value = jnp.sum(radial * at_stars, axis=0)
    pair = lax.psum(partial_value, "core")
    predicted = jnp.sum(lax.all_gather(pair, "zhi"), axis=0)
    weight_back = (predicted - observed) / (sigma * sigma)

    adjoint_sum = lax.dot_general(
        radial * weight_back[None, :],
        spread,
        (((1,), (1,)), ((), ())),
        precision=HIGHEST,
        preferred_element_type=jnp.float32,
    )
    sensitivity = adjoint_sum * weighted

    terms = stencil[:, :, None] * sensitivity[:, None, :]
    framed = spread_select(terms, pick)
    to_after, to_before = lax.optimization_barrier((framed[:, frame - COLS :], framed[:, :COLS]))
    from_before = ring(to_after, "ang", 1)
    from_after = ring(to_before, "ang", -1)
    inner = framed[:, COLS : frame - COLS]
    gradient = jnp.concatenate(
        [inner[:, :COLS] + from_before, inner[:, COLS : pixels - COLS], inner[:, pixels - COLS :] + from_after],
        axis=1,
    )
    return (predicted, gradient)


def solution(mesh):
    ang, rad = mesh.devices.shape
    split = Mesh(mesh.devices.reshape(ang, rad // 2, 2), ("ang", "zhi", "core"))
    shell = ("zhi", "core")
    return jax.shard_map(
        on_device,
        mesh=split,
        in_specs=(
            P(shell, "ang"),
            P(shell, None),
            P(shell),
            P(None, "ang"),
            P("ang"),
            P(None, "ang"),
            P(None, "ang"),
            P("ang"),
            P("ang"),
            P("ang"),
        ),
        out_specs=(P("ang"), P(shell, "ang")),
        check_vma=False,
    )
```

```python
import jax
import jax.numpy as jnp
from jax import lax
from jax.sharding import Mesh, PartitionSpec as P

COLS = 128
HIGHEST = lax.Precision.HIGHEST


def split3(value):
    high = lax.reduce_precision(value, exponent_bits=8, mantissa_bits=7)
    rest = value - high
    middle = lax.reduce_precision(rest, exponent_bits=8, mantissa_bits=7)
    low = rest - middle
    return jnp.concatenate([high, middle, low], axis=0).astype(jnp.bfloat16)


def select(value, onehot):
    rows = value.shape[0]
    product = lax.dot_general(split3(value), onehot, (((1,), (0,)), ((), ())), preferred_element_type=jnp.float32)
    return product[:rows] + product[rows : 2 * rows] + product[2 * rows :]


def spread_select(value, onehot):
    rows = value.shape[0]
    product = lax.dot_general(
        split3(value), onehot, (((1, 2), (1, 2)), ((), ())), preferred_element_type=jnp.float32
    )
    return product[:rows] + product[rows : 2 * rows] + product[2 * rows :]


def chip_sum(value, axis):
    count = lax.axis_size(axis)
    if count != 4:
        return jnp.sum(lax.all_gather(value, axis), axis=0)
    from_next = ring(value, axis, -1)
    from_prev = ring(value, axis, 1)
    opposite = ring(from_next, axis, -1)
    relative = jnp.stack([value, from_next, opposite, from_prev])
    ordered = jnp.roll(relative, lax.axis_index(axis), axis=0)
    return jnp.sum(ordered, axis=0)


def ring(value, axis, step):
    count = lax.axis_size(axis)
    return lax.ppermute(value, axis, [(i, (i + step) % count) for i in range(count)])


def on_device(
    latent,
    stencil,
    bin_width,
    neighbours,
    star_bin,
    star_pixels,
    star_weights,
    star_frac,
    observed,
    sigma,
):
    shells, pixels = latent.shape
    taps = neighbours.shape[0]
    frame = pixels + 2 * COLS

    before = ring(latent, "ang", 1)
    after = ring(latent, "ang", -1)
    wide = jnp.concatenate([before[:, pixels - COLS :], latent, after[:, :COLS]], axis=1)

    position = lax.broadcasted_iota(jnp.int32, (frame, taps, pixels), 0)
    pick = (position == neighbours[None, :, :]).astype(jnp.bfloat16)
    picked = select(wide, pick)
    refined = jnp.sum(picked * stencil[:, :, None], axis=1)
    density = jnp.exp(refined)
    weighted = bin_width[:, None] * density

    nstars = star_bin.shape[0]
    pixel_id = lax.broadcasted_iota(jnp.int32, (pixels, nstars), 0)
    spread = jnp.sum(jnp.where(pixel_id[None] == star_pixels[:, None, :], star_weights[:, None, :], 0.0), axis=0)

    shell_start = (lax.axis_index("zhi") * lax.axis_size("core") + lax.axis_index("core")) * shells
    bin_id = shell_start + lax.broadcasted_iota(jnp.int32, (shells, nstars), 0)
    lower = star_bin[None, :]
    radial = jnp.where(bin_id <= lower, 1.0, jnp.where(bin_id - 1 == lower, star_frac[None, :], 0.0))

    at_stars = jnp.dot(weighted, spread, precision=HIGHEST, preferred_element_type=jnp.float32)
    partial_value = jnp.sum(radial * at_stars, axis=0)
    pair = lax.psum(partial_value, "core")
    predicted = chip_sum(pair, "zhi")
    weight_back = (predicted - observed) / (sigma * sigma)

    adjoint_sum = lax.dot_general(
        radial * weight_back[None, :],
        spread,
        (((1,), (1,)), ((), ())),
        precision=HIGHEST,
        preferred_element_type=jnp.float32,
    )
    sensitivity = adjoint_sum * weighted

    terms = stencil[:, :, None] * sensitivity[:, None, :]
    framed = spread_select(terms, pick)
    to_after, to_before = lax.optimization_barrier((framed[:, frame - COLS :], framed[:, :COLS]))
    from_before = ring(to_after, "ang", 1)
    from_after = ring(to_before, "ang", -1)
    inner = framed[:, COLS : frame - COLS]
    gradient = jnp.concatenate(
        [inner[:, :COLS] + from_before, inner[:, COLS : pixels - COLS], inner[:, pixels - COLS :] + from_after],
        axis=1,
    )
    return (predicted, gradient)


def solution(mesh):
    ang, rad = mesh.devices.shape
    split = Mesh(mesh.devices.reshape(ang, rad // 2, 2), ("ang", "zhi", "core"))
    shell = ("zhi", "core")
    return jax.shard_map(
        on_device,
        mesh=split,
        in_specs=(
            P(shell, "ang"),
            P(shell, None),
            P(shell),
            P(None, "ang"),
            P("ang"),
            P(None, "ang"),
            P(None, "ang"),
            P("ang"),
            P("ang"),
            P("ang"),
        ),
        out_specs=(P("ang"), P(shell, "ang")),
        check_vma=False,
    )
```

```python
import jax
import jax.numpy as jnp
from jax import lax
from jax.sharding import Mesh, PartitionSpec as P

COLS = 128
HIGHEST = lax.Precision.HIGHEST


def split3(value, axis):
    high = lax.reduce_precision(value, exponent_bits=8, mantissa_bits=7)
    rest = value - high
    middle = lax.reduce_precision(rest, exponent_bits=8, mantissa_bits=7)
    low = rest - middle
    return jnp.concatenate([high, middle, low], axis=axis).astype(jnp.bfloat16)


def select(value, table):
    frame = value.shape[1]
    position = lax.broadcasted_iota(jnp.int32, (3 * frame,) + table.shape, 0) % frame
    onehot = (position == table[None]).astype(jnp.bfloat16)
    return lax.dot_general(split3(value, 1), onehot, (((1,), (0,)), ((), ())), preferred_element_type=jnp.float32)


def spread_select(value, table, frame):
    tiled = jnp.concatenate([table] * 3, axis=0)
    position = lax.broadcasted_iota(jnp.int32, (frame,) + tiled.shape, 0)
    onehot = (position == tiled[None]).astype(jnp.bfloat16)
    return lax.dot_general(
        split3(value, 1), onehot, (((1, 2), (1, 2)), ((), ())), preferred_element_type=jnp.float32
    )


def chip_sum(value, axis):
    count = lax.axis_size(axis)
    if count != 4:
        return jnp.sum(lax.all_gather(value, axis), axis=0)
    from_next = ring(value, axis, -1)
    from_prev = ring(value, axis, 1)
    opposite = ring(from_next, axis, -1)
    relative = jnp.stack([value, from_next, opposite, from_prev])
    ordered = jnp.roll(relative, lax.axis_index(axis), axis=0)
    return jnp.sum(ordered, axis=0)


def ring(value, axis, step):
    count = lax.axis_size(axis)
    return lax.ppermute(value, axis, [(i, (i + step) % count) for i in range(count)])


def on_device(
    latent,
    stencil,
    bin_width,
    neighbours,
    star_bin,
    star_pixels,
    star_weights,
    star_frac,
    observed,
    sigma,
):
    shells, pixels = latent.shape
    taps = neighbours.shape[0]
    frame = pixels + 2 * COLS

    before = ring(latent, "ang", 1)
    after = ring(latent, "ang", -1)
    wide = jnp.concatenate([before[:, pixels - COLS :], latent, after[:, :COLS]], axis=1)

    picked = select(wide, neighbours)
    refined = jnp.sum(picked * stencil[:, :, None], axis=1)
    density = jnp.exp(refined)
    weighted = bin_width[:, None] * density

    nstars = star_bin.shape[0]
    pixel_id = lax.broadcasted_iota(jnp.int32, (pixels, nstars), 0)
    spread = jnp.sum(jnp.where(pixel_id[None] == star_pixels[:, None, :], star_weights[:, None, :], 0.0), axis=0)

    shell_start = (lax.axis_index("zhi") * lax.axis_size("core") + lax.axis_index("core")) * shells
    bin_id = shell_start + lax.broadcasted_iota(jnp.int32, (shells, nstars), 0)
    lower = star_bin[None, :]
    radial = jnp.where(bin_id <= lower, 1.0, jnp.where(bin_id - 1 == lower, star_frac[None, :], 0.0))

    at_stars = jnp.dot(weighted, spread, precision=HIGHEST, preferred_element_type=jnp.float32)
    partial_value = jnp.sum(radial * at_stars, axis=0)
    pair = lax.psum(partial_value, "core")
    predicted = chip_sum(pair, "zhi")
    weight_back = (predicted - observed) / (sigma * sigma)

    adjoint_sum = lax.dot_general(
        radial * weight_back[None, :],
        spread,
        (((1,), (1,)), ((), ())),
        precision=HIGHEST,
        preferred_element_type=jnp.float32,
    )
    sensitivity = adjoint_sum * weighted

    terms = stencil[:, :, None] * sensitivity[:, None, :]
    framed = spread_select(terms, neighbours, frame)
    to_after, to_before = lax.optimization_barrier((framed[:, frame - COLS :], framed[:, :COLS]))
    from_before = ring(to_after, "ang", 1)
    from_after = ring(to_before, "ang", -1)
    inner = framed[:, COLS : frame - COLS]
    gradient = jnp.concatenate(
        [inner[:, :COLS] + from_before, inner[:, COLS : pixels - COLS], inner[:, pixels - COLS :] + from_after],
        axis=1,
    )
    return (predicted, gradient)


def solution(mesh):
    ang, rad = mesh.devices.shape
    split = Mesh(mesh.devices.reshape(ang, rad // 2, 2), ("ang", "zhi", "core"))
    shell = ("zhi", "core")
    return jax.shard_map(
        on_device,
        mesh=split,
        in_specs=(
            P(shell, "ang"),
            P(shell, None),
            P(shell),
            P(None, "ang"),
            P("ang"),
            P(None, "ang"),
            P(None, "ang"),
            P("ang"),
            P("ang"),
            P("ang"),
        ),
        out_specs=(P("ang"), P(shell, "ang")),
        check_vma=False,
    )
```

```python
import jax
import jax.numpy as jnp
from jax import lax
from jax.sharding import Mesh, PartitionSpec as P

COLS = 128
HIGHEST = lax.Precision.HIGHEST


def split3(value):
    high = lax.reduce_precision(value, exponent_bits=8, mantissa_bits=7)
    rest = value - high
    middle = lax.reduce_precision(rest, exponent_bits=8, mantissa_bits=7)
    low = rest - middle
    return jnp.concatenate([high, middle, low], axis=0).astype(jnp.bfloat16)


def select(value, onehot):
    rows = value.shape[0]
    product = lax.dot_general(split3(value), onehot, (((1,), (0,)), ((), ())), preferred_element_type=jnp.float32)
    return product[:rows] + product[rows : 2 * rows] + product[2 * rows :]


def spread_select(value, onehot):
    rows = value.shape[0]
    product = lax.dot_general(
        split3(value), onehot, (((1, 2), (1, 2)), ((), ())), preferred_element_type=jnp.float32
    )
    return product[:rows] + product[rows : 2 * rows] + product[2 * rows :]


def chip_sum(value, axis):
    count = lax.axis_size(axis)
    if count != 4:
        return jnp.sum(lax.all_gather(value, axis), axis=0)
    from_next = ring(value, axis, -1)
    from_prev = ring(value, axis, 1)
    opposite = ring(from_next, axis, -1)
    relative = jnp.stack([value, from_next, opposite, from_prev])
    ordered = jnp.roll(relative, lax.axis_index(axis), axis=0)
    return jnp.sum(ordered, axis=0)


def ring(value, axis, step):
    count = lax.axis_size(axis)
    return lax.ppermute(value, axis, [(i, (i + step) % count) for i in range(count)])


def on_device(
    latent,
    stencil,
    bin_width,
    neighbours,
    star_bin,
    star_pixels,
    star_weights,
    star_frac,
    observed,
    sigma,
):
    shells, pixels = latent.shape
    taps = neighbours.shape[0]
    frame = pixels + 2 * COLS

    before = ring(latent, "ang", 1)
    after = ring(latent, "ang", -1)
    wide = jnp.concatenate([before[:, pixels - COLS :], latent, after[:, :COLS]], axis=1)

    position = lax.broadcasted_iota(jnp.int32, (frame, taps, pixels), 0)
    pick = (position == neighbours[None, :, :]).astype(jnp.bfloat16)
    picked = select(wide, pick)
    refined = jnp.sum(picked * stencil[:, :, None], axis=1)
    density = jnp.exp(refined)
    weighted = bin_width[:, None] * density

    nstars = star_bin.shape[0]
    pixel_id = lax.broadcasted_iota(jnp.int32, (pixels, nstars), 0)
    spread = jnp.sum(jnp.where(pixel_id[None] == star_pixels[:, None, :], star_weights[:, None, :], 0.0), axis=0)

    shell_start = (lax.axis_index("zhi") * lax.axis_size("core") + lax.axis_index("core")) * shells
    bin_id = shell_start + lax.broadcasted_iota(jnp.int32, (shells, nstars), 0)
    lower = star_bin[None, :]
    radial = jnp.where(bin_id <= lower, 1.0, jnp.where(bin_id - 1 == lower, star_frac[None, :], 0.0))

    at_stars = jnp.dot(weighted, spread, precision=HIGHEST, preferred_element_type=jnp.float32)
    partial_value = jnp.sum(radial * at_stars, axis=0)
    pair = lax.psum(partial_value, "core")
    predicted = chip_sum(pair, "zhi")
    weight_back = (predicted - observed) / (sigma * sigma)

    adjoint_sum = lax.dot_general(
        radial * weight_back[None, :],
        spread,
        (((1,), (1,)), ((), ())),
        precision=HIGHEST,
        preferred_element_type=jnp.float32,
    )
    sensitivity = adjoint_sum * weighted

    terms = stencil[:, :, None] * sensitivity[:, None, :]
    edge_id = lax.broadcasted_iota(jnp.int32, (2 * COLS, taps, pixels), 0)
    edge_id = edge_id + jnp.where(edge_id >= COLS, frame - 2 * COLS, 0)
    edges = spread_select(terms, (edge_id == neighbours[None]).astype(jnp.bfloat16))
    to_after, to_before = lax.optimization_barrier((edges[:, COLS:], edges[:, :COLS]))
    from_before = ring(to_after, "ang", 1)
    from_after = ring(to_before, "ang", -1)
    own_id = COLS + lax.broadcasted_iota(jnp.int32, (pixels, taps, pixels), 0)
    inner = spread_select(terms, (own_id == neighbours[None]).astype(jnp.bfloat16))
    gradient = inner + jnp.pad(from_before, ((0, 0), (0, pixels - COLS))) + jnp.pad(
        from_after, ((0, 0), (pixels - COLS, 0))
    )
    return (predicted, gradient)


def solution(mesh):
    ang, rad = mesh.devices.shape
    split = Mesh(mesh.devices.reshape(ang, rad // 2, 2), ("ang", "zhi", "core"))
    shell = ("zhi", "core")
    return jax.shard_map(
        on_device,
        mesh=split,
        in_specs=(
            P(shell, "ang"),
            P(shell, None),
            P(shell),
            P(None, "ang"),
            P("ang"),
            P(None, "ang"),
            P(None, "ang"),
            P("ang"),
            P("ang"),
            P("ang"),
        ),
        out_specs=(P("ang"), P(shell, "ang")),
        check_vma=False,
    )
```

```python
import jax
import jax.numpy as jnp
from jax import lax
from jax.sharding import Mesh, PartitionSpec as P

COLS = 128
HIGHEST = lax.Precision.HIGHEST


def split3(value):
    high = lax.reduce_precision(value, exponent_bits=8, mantissa_bits=7)
    rest = value - high
    middle = lax.reduce_precision(rest, exponent_bits=8, mantissa_bits=7)
    low = rest - middle
    return jnp.concatenate([high, middle, low], axis=0).astype(jnp.bfloat16)


def select(value, onehot):
    rows = value.shape[0]
    product = lax.dot_general(split3(value), onehot, (((1,), (0,)), ((), ())), preferred_element_type=jnp.float32)
    return product[:rows] + product[rows : 2 * rows] + product[2 * rows :]


def spread_select(value, onehot):
    rows = value.shape[0]
    product = lax.dot_general(
        split3(value), onehot, (((1, 2), (1, 2)), ((), ())), preferred_element_type=jnp.float32
    )
    return product[:rows] + product[rows : 2 * rows] + product[2 * rows :]


def ring(value, axis, step):
    count = lax.axis_size(axis)
    return lax.ppermute(value, axis, [(i, (i + step) % count) for i in range(count)])


def on_device(
    latent,
    stencil,
    bin_width,
    neighbours,
    star_bin,
    star_pixels,
    star_weights,
    star_frac,
    observed,
    sigma,
):
    shells, pixels = latent.shape
    taps = neighbours.shape[0]
    frame = pixels + 2 * COLS

    before = ring(latent, "ang", 1)
    after = ring(latent, "ang", -1)
    wide = jnp.concatenate([before[:, pixels - COLS :], latent, after[:, :COLS]], axis=1)

    position = lax.broadcasted_iota(jnp.int32, (frame, taps, pixels), 0)
    pick = (position == neighbours[None, :, :]).astype(jnp.bfloat16)
    picked = select(wide, pick)
    refined = jnp.sum(picked * stencil[:, :, None], axis=1)
    density = jnp.exp(refined)
    weighted = bin_width[:, None] * density

    nstars = star_bin.shape[0]
    pixel_id = lax.broadcasted_iota(jnp.int32, (pixels, nstars), 0)
    spread = jnp.sum(jnp.where(pixel_id[None] == star_pixels[:, None, :], star_weights[:, None, :], 0.0), axis=0)

    shell_start = (lax.axis_index("zhi") * lax.axis_size("core") + lax.axis_index("core")) * shells
    bin_id = shell_start + lax.broadcasted_iota(jnp.int32, (shells, nstars), 0)
    lower = star_bin[None, :]
    radial = jnp.where(bin_id <= lower, 1.0, jnp.where(bin_id - 1 == lower, star_frac[None, :], 0.0))

    at_stars = jnp.dot(weighted, spread, precision=HIGHEST, preferred_element_type=jnp.float32)
    partial_value = jnp.sum(radial * at_stars, axis=0)
    pair = lax.psum(partial_value, "core")
    predicted = jnp.sum(lax.all_gather(pair, "zhi"), axis=0)
    weight_back = (predicted - observed) / (sigma * sigma)

    adjoint_sum = lax.dot_general(
        radial * weight_back[None, :],
        spread,
        (((1,), (1,)), ((), ())),
        precision=HIGHEST,
        preferred_element_type=jnp.float32,
    )
    sensitivity = adjoint_sum * weighted

    terms = stencil[:, :, None] * sensitivity[:, None, :]
    edge_id = lax.broadcasted_iota(jnp.int32, (2 * COLS, taps, pixels), 0)
    edge_id = edge_id + jnp.where(edge_id >= COLS, frame - 2 * COLS, 0)
    edges = spread_select(terms, (edge_id == neighbours[None]).astype(jnp.bfloat16))
    to_after, to_before = lax.optimization_barrier((edges[:, COLS:], edges[:, :COLS]))
    from_before = ring(to_after, "ang", 1)
    from_after = ring(to_before, "ang", -1)
    own_id = COLS + lax.broadcasted_iota(jnp.int32, (pixels, taps, pixels), 0)
    inner = spread_select(terms, (own_id == neighbours[None]).astype(jnp.bfloat16))
    gradient = inner + jnp.pad(from_before, ((0, 0), (0, pixels - COLS))) + jnp.pad(
        from_after, ((0, 0), (pixels - COLS, 0))
    )
    return (predicted, gradient)


def solution(mesh):
    ang, rad = mesh.devices.shape
    split = Mesh(mesh.devices.reshape(ang, rad // 2, 2), ("ang", "zhi", "core"))
    shell = ("zhi", "core")
    return jax.shard_map(
        on_device,
        mesh=split,
        in_specs=(
            P(shell, "ang"),
            P(shell, None),
            P(shell),
            P(None, "ang"),
            P("ang"),
            P(None, "ang"),
            P(None, "ang"),
            P("ang"),
            P("ang"),
            P("ang"),
        ),
        out_specs=(P("ang"), P(shell, "ang")),
        check_vma=False,
    )
```

```python
import jax
import jax.numpy as jnp
from jax import lax
from jax.sharding import Mesh, PartitionSpec as P

COLS = 128
HIGHEST = lax.Precision.HIGHEST


def split3(value):
    high = lax.reduce_precision(value, exponent_bits=8, mantissa_bits=7)
    rest = value - high
    middle = lax.reduce_precision(rest, exponent_bits=8, mantissa_bits=7)
    low = rest - middle
    return jnp.concatenate([high, middle, low], axis=0).astype(jnp.bfloat16)


def select(value, onehot):
    rows = value.shape[0]
    product = lax.dot_general(split3(value), onehot, (((1,), (0,)), ((), ())), preferred_element_type=jnp.float32)
    return product[:rows] + product[rows : 2 * rows] + product[2 * rows :]


def spread_select(value, onehot):
    rows = value.shape[0]
    product = lax.dot_general(
        split3(value), onehot, (((1, 2), (1, 2)), ((), ())), preferred_element_type=jnp.float32
    )
    return product[:rows] + product[rows : 2 * rows] + product[2 * rows :]


def shell_sum(value):
    chips, cores = lax.axis_size("zhi"), lax.axis_size("core")
    if chips != 4 or cores != 2:
        return jnp.sum(lax.all_gather(value, ("zhi", "core")), axis=0)
    swap = [(0, 1), (1, 0)]
    from_next = ring(value, "zhi", -1)
    from_prev = ring(value, "zhi", 1)
    from_core = lax.ppermute(value, "core", swap)
    opposite = ring(from_next, "zhi", -1)
    core_sides = lax.ppermute(jnp.stack([from_next, from_prev]), "core", swap)
    diagonal = [(j * 2 + d, ((j - 1) % chips) * 2 + (1 - d)) for j in range(chips) for d in range(cores)]
    core_opposite = lax.ppermute(from_next, ("zhi", "core"), diagonal)
    chip = lax.axis_index("zhi")
    own = jnp.roll(jnp.stack([value, from_next, opposite, from_prev]), chip, axis=0)
    other = jnp.roll(jnp.stack([from_core, core_sides[0], core_opposite, core_sides[1]]), chip, axis=0)
    first = lax.axis_index("core") == 0
    ordered = jnp.stack([jnp.where(first, own, other), jnp.where(first, other, own)], axis=1)
    return jnp.sum(ordered.reshape(chips * cores, -1), axis=0)


def ring(value, axis, step):
    count = lax.axis_size(axis)
    return lax.ppermute(value, axis, [(i, (i + step) % count) for i in range(count)])


def on_device(
    latent,
    stencil,
    bin_width,
    neighbours,
    star_bin,
    star_pixels,
    star_weights,
    star_frac,
    observed,
    sigma,
):
    shells, pixels = latent.shape
    taps = neighbours.shape[0]
    frame = pixels + 2 * COLS

    before = ring(latent, "ang", 1)
    after = ring(latent, "ang", -1)
    wide = jnp.concatenate([before[:, pixels - COLS :], latent, after[:, :COLS]], axis=1)

    position = lax.broadcasted_iota(jnp.int32, (frame, taps, pixels), 0)
    pick = (position == neighbours[None, :, :]).astype(jnp.bfloat16)
    picked = select(wide, pick)
    refined = jnp.sum(picked * stencil[:, :, None], axis=1)
    density = jnp.exp(refined)
    weighted = bin_width[:, None] * density

    nstars = star_bin.shape[0]
    pixel_id = lax.broadcasted_iota(jnp.int32, (pixels, nstars), 0)
    spread = jnp.sum(jnp.where(pixel_id[None] == star_pixels[:, None, :], star_weights[:, None, :], 0.0), axis=0)

    shell_start = (lax.axis_index("zhi") * lax.axis_size("core") + lax.axis_index("core")) * shells
    bin_id = shell_start + lax.broadcasted_iota(jnp.int32, (shells, nstars), 0)
    lower = star_bin[None, :]
    radial = jnp.where(bin_id <= lower, 1.0, jnp.where(bin_id - 1 == lower, star_frac[None, :], 0.0))

    at_stars = jnp.dot(weighted, spread, precision=HIGHEST, preferred_element_type=jnp.float32)
    partial_value = jnp.sum(radial * at_stars, axis=0)
    predicted = shell_sum(partial_value)
    weight_back = (predicted - observed) / (sigma * sigma)

    adjoint_sum = lax.dot_general(
        radial * weight_back[None, :],
        spread,
        (((1,), (1,)), ((), ())),
        precision=HIGHEST,
        preferred_element_type=jnp.float32,
    )
    sensitivity = adjoint_sum * weighted

    terms = stencil[:, :, None] * sensitivity[:, None, :]
    edge_id = lax.broadcasted_iota(jnp.int32, (2 * COLS, taps, pixels), 0)
    edge_id = edge_id + jnp.where(edge_id >= COLS, frame - 2 * COLS, 0)
    edges = spread_select(terms, (edge_id == neighbours[None]).astype(jnp.bfloat16))
    to_after, to_before = lax.optimization_barrier((edges[:, COLS:], edges[:, :COLS]))
    from_before = ring(to_after, "ang", 1)
    from_after = ring(to_before, "ang", -1)
    own_id = COLS + lax.broadcasted_iota(jnp.int32, (pixels, taps, pixels), 0)
    inner = spread_select(terms, (own_id == neighbours[None]).astype(jnp.bfloat16))
    gradient = inner + jnp.pad(from_before, ((0, 0), (0, pixels - COLS))) + jnp.pad(
        from_after, ((0, 0), (pixels - COLS, 0))
    )
    return (predicted, gradient)


def solution(mesh):
    ang, rad = mesh.devices.shape
    split = Mesh(mesh.devices.reshape(ang, rad // 2, 2), ("ang", "zhi", "core"))
    shell = ("zhi", "core")
    return jax.shard_map(
        on_device,
        mesh=split,
        in_specs=(
            P(shell, "ang"),
            P(shell, None),
            P(shell),
            P(None, "ang"),
            P("ang"),
            P(None, "ang"),
            P(None, "ang"),
            P("ang"),
            P("ang"),
            P("ang"),
        ),
        out_specs=(P("ang"), P(shell, "ang")),
        check_vma=False,
    )
```

```python
import jax
import jax.numpy as jnp
from jax import lax
from jax.sharding import Mesh, PartitionSpec as P

COLS = 128
HIGHEST = lax.Precision.HIGHEST


def split3(value):
    high = lax.reduce_precision(value, exponent_bits=8, mantissa_bits=7)
    rest = value - high
    middle = lax.reduce_precision(rest, exponent_bits=8, mantissa_bits=7)
    low = rest - middle
    return jnp.concatenate([high, middle, low], axis=0).astype(jnp.bfloat16)


def select(value, onehot):
    rows = value.shape[0]
    product = lax.dot_general(split3(value), onehot, (((1,), (0,)), ((), ())), preferred_element_type=jnp.float32)
    return product[:rows] + product[rows : 2 * rows] + product[2 * rows :]


def spread_select(value, onehot):
    rows = value.shape[0]
    product = lax.dot_general(
        split3(value), onehot, (((1, 2), (1, 2)), ((), ())), preferred_element_type=jnp.float32
    )
    return product[:rows] + product[rows : 2 * rows] + product[2 * rows :]


def chip_sum(value, axis):
    count = lax.axis_size(axis)
    if count != 4:
        return jnp.sum(lax.all_gather(value, axis), axis=0)
    from_next = ring(value, axis, -1)
    from_prev = ring(value, axis, 1)
    opposite = ring(from_next, axis, -1)
    relative = jnp.stack([value, from_next, opposite, from_prev])
    ordered = jnp.roll(relative, lax.axis_index(axis), axis=0)
    return jnp.sum(ordered, axis=0)


def ring(value, axis, step):
    count = lax.axis_size(axis)
    return lax.ppermute(value, axis, [(i, (i + step) % count) for i in range(count)])


def on_device(
    latent,
    stencil,
    bin_width,
    neighbours,
    star_bin,
    star_pixels,
    star_weights,
    star_frac,
    observed,
    sigma,
):
    shells, pixels = latent.shape
    taps = neighbours.shape[0]
    frame = pixels + 2 * COLS

    before = ring(latent, "ang", 1)
    after = ring(latent, "ang", -1)
    wide = jnp.concatenate([before[:, pixels - COLS :], latent, after[:, :COLS]], axis=1)

    position = lax.broadcasted_iota(jnp.int32, (frame, taps, pixels), 0)
    pick = (position == neighbours[None, :, :]).astype(jnp.bfloat16)
    picked = select(wide, pick)
    refined = jnp.sum(picked * stencil[:, :, None], axis=1)
    density = jnp.exp(refined)
    weighted = bin_width[:, None] * density

    nstars = star_bin.shape[0]
    pixel_id = lax.broadcasted_iota(jnp.int32, (pixels, nstars), 0)
    spread = jnp.sum(jnp.where(pixel_id[None] == star_pixels[:, None, :], star_weights[:, None, :], 0.0), axis=0)

    shell_start = (lax.axis_index("zhi") * lax.axis_size("core") + lax.axis_index("core")) * shells
    bin_id = shell_start + lax.broadcasted_iota(jnp.int32, (shells, nstars), 0)
    lower = star_bin[None, :]
    radial = jnp.where(bin_id <= lower, 1.0, jnp.where(bin_id - 1 == lower, star_frac[None, :], 0.0))

    at_stars = jnp.dot(weighted, spread, precision=HIGHEST, preferred_element_type=jnp.float32)
    partial_value = jnp.sum(radial * at_stars, axis=0)
    pair = lax.psum(partial_value, "core")
    predicted = chip_sum(pair, "zhi")
    weight_back = (predicted - observed) / (sigma * sigma)

    spread_parts = lax.optimization_barrier(split3(spread))
    spread_parts = spread_parts.reshape(3 * pixels, nstars)
    blocks = lax.dot_general(
        split3(radial * weight_back[None, :]),
        spread_parts,
        (((1,), (1,)), ((), ())),
        preferred_element_type=jnp.float32,
    )
    part = lambda i, j: blocks[i * shells : (i + 1) * shells, j * pixels : (j + 1) * pixels]
    adjoint_sum = ((part(2, 0) + part(0, 2)) + part(1, 1)) + (part(1, 0) + part(0, 1)) + part(0, 0)
    sensitivity = adjoint_sum * weighted

    terms = stencil[:, :, None] * sensitivity[:, None, :]
    edge_id = lax.broadcasted_iota(jnp.int32, (2 * COLS, taps, pixels), 0)
    edge_id = edge_id + jnp.where(edge_id >= COLS, frame - 2 * COLS, 0)
    edges = spread_select(terms, (edge_id == neighbours[None]).astype(jnp.bfloat16))
    to_after, to_before = lax.optimization_barrier((edges[:, COLS:], edges[:, :COLS]))
    from_before = ring(to_after, "ang", 1)
    from_after = ring(to_before, "ang", -1)
    own_id = COLS + lax.broadcasted_iota(jnp.int32, (pixels, taps, pixels), 0)
    inner = spread_select(terms, (own_id == neighbours[None]).astype(jnp.bfloat16))
    gradient = inner + jnp.pad(from_before, ((0, 0), (0, pixels - COLS))) + jnp.pad(
        from_after, ((0, 0), (pixels - COLS, 0))
    )
    return (predicted, gradient)


def solution(mesh):
    ang, rad = mesh.devices.shape
    split = Mesh(mesh.devices.reshape(ang, rad // 2, 2), ("ang", "zhi", "core"))
    shell = ("zhi", "core")
    return jax.shard_map(
        on_device,
        mesh=split,
        in_specs=(
            P(shell, "ang"),
            P(shell, None),
            P(shell),
            P(None, "ang"),
            P("ang"),
            P(None, "ang"),
            P(None, "ang"),
            P("ang"),
            P("ang"),
            P("ang"),
        ),
        out_specs=(P("ang"), P(shell, "ang")),
        check_vma=False,
    )
```

```python
import jax
import jax.numpy as jnp
from jax import lax
from jax.sharding import Mesh, PartitionSpec as P

COLS = 128
HIGHEST = lax.Precision.HIGHEST


def split3(value):
    high = lax.reduce_precision(value, exponent_bits=8, mantissa_bits=7)
    rest = value - high
    middle = lax.reduce_precision(rest, exponent_bits=8, mantissa_bits=7)
    low = rest - middle
    return jnp.concatenate([high, middle, low], axis=0).astype(jnp.bfloat16)


def select(value, onehot):
    rows = value.shape[0]
    product = lax.dot_general(split3(value), onehot, (((1,), (0,)), ((), ())), preferred_element_type=jnp.float32)
    return product[:rows] + product[rows : 2 * rows] + product[2 * rows :]


def spread_select(value, onehot):
    rows = value.shape[0]
    product = lax.dot_general(
        split3(value), onehot, (((1, 2), (1, 2)), ((), ())), preferred_element_type=jnp.float32
    )
    return product[:rows] + product[rows : 2 * rows] + product[2 * rows :]


def chip_sum(value, axis):
    count = lax.axis_size(axis)
    if count != 4:
        return jnp.sum(lax.all_gather(value, axis), axis=0)
    from_next = ring(value, axis, -1)
    from_prev = ring(value, axis, 1)
    opposite = ring(from_next, axis, -1)
    relative = jnp.stack([value, from_next, opposite, from_prev])
    ordered = jnp.roll(relative, lax.axis_index(axis), axis=0)
    return jnp.sum(ordered, axis=0)


def ring(value, axis, step):
    count = lax.axis_size(axis)
    return lax.ppermute(value, axis, [(i, (i + step) % count) for i in range(count)])


def on_device(
    latent,
    stencil,
    bin_width,
    neighbours,
    star_bin,
    star_pixels,
    star_weights,
    star_frac,
    observed,
    sigma,
):
    shells, pixels = latent.shape
    taps = neighbours.shape[0]
    frame = pixels + 2 * COLS

    before = ring(latent, "ang", 1)
    after = ring(latent, "ang", -1)
    wide = jnp.concatenate([before[:, pixels - COLS :], latent, after[:, :COLS]], axis=1)

    position = lax.broadcasted_iota(jnp.int32, (frame, taps, pixels), 0)
    pick = (position == neighbours[None, :, :]).astype(jnp.bfloat16)
    picked = select(wide, pick)
    refined = jnp.sum(picked * stencil[:, :, None], axis=1)
    density = jnp.exp(refined)
    weighted = bin_width[:, None] * density

    nstars = star_bin.shape[0]
    pixel_id = lax.broadcasted_iota(jnp.int32, (pixels, nstars), 0)
    spread = jnp.zeros((pixels, nstars), jnp.float32)
    for corner in range(star_pixels.shape[0]):
        spread = spread + jnp.where(pixel_id == star_pixels[corner][None, :], star_weights[corner][None, :], 0.0)
    spread = lax.optimization_barrier(spread)

    shell_start = (lax.axis_index("zhi") * lax.axis_size("core") + lax.axis_index("core")) * shells
    bin_id = shell_start + lax.broadcasted_iota(jnp.int32, (shells, nstars), 0)
    lower = star_bin[None, :]
    radial = jnp.where(bin_id <= lower, 1.0, jnp.where(bin_id - 1 == lower, star_frac[None, :], 0.0))

    at_stars = jnp.dot(weighted, spread, precision=HIGHEST, preferred_element_type=jnp.float32)
    partial_value = jnp.sum(radial * at_stars, axis=0)
    pair = lax.psum(partial_value, "core")
    predicted = chip_sum(pair, "zhi")
    weight_back = (predicted - observed) / (sigma * sigma)

    adjoint_sum = lax.dot_general(
        radial * weight_back[None, :],
        spread,
        (((1,), (1,)), ((), ())),
        precision=HIGHEST,
        preferred_element_type=jnp.float32,
    )
    sensitivity = adjoint_sum * weighted

    terms = stencil[:, :, None] * sensitivity[:, None, :]
    edge_id = lax.broadcasted_iota(jnp.int32, (2 * COLS, taps, pixels), 0)
    edge_id = edge_id + jnp.where(edge_id >= COLS, frame - 2 * COLS, 0)
    edges = spread_select(terms, (edge_id == neighbours[None]).astype(jnp.bfloat16))
    to_after, to_before = lax.optimization_barrier((edges[:, COLS:], edges[:, :COLS]))
    from_before = ring(to_after, "ang", 1)
    from_after = ring(to_before, "ang", -1)
    own_id = COLS + lax.broadcasted_iota(jnp.int32, (pixels, taps, pixels), 0)
    inner = spread_select(terms, (own_id == neighbours[None]).astype(jnp.bfloat16))
    gradient = inner + jnp.pad(from_before, ((0, 0), (0, pixels - COLS))) + jnp.pad(
        from_after, ((0, 0), (pixels - COLS, 0))
    )
    return (predicted, gradient)


def solution(mesh):
    ang, rad = mesh.devices.shape
    split = Mesh(mesh.devices.reshape(ang, rad // 2, 2), ("ang", "zhi", "core"))
    shell = ("zhi", "core")
    return jax.shard_map(
        on_device,
        mesh=split,
        in_specs=(
            P(shell, "ang"),
            P(shell, None),
            P(shell),
            P(None, "ang"),
            P("ang"),
            P(None, "ang"),
            P(None, "ang"),
            P("ang"),
            P("ang"),
            P("ang"),
        ),
        out_specs=(P("ang"), P(shell, "ang")),
        check_vma=False,
    )
```

```python
import jax
import jax.numpy as jnp
from jax import lax
from jax.sharding import Mesh, PartitionSpec as P

COLS = 128
HIGHEST = lax.Precision.HIGHEST


def split3(value):
    high = lax.reduce_precision(value, exponent_bits=8, mantissa_bits=7)
    rest = value - high
    middle = lax.reduce_precision(rest, exponent_bits=8, mantissa_bits=7)
    low = rest - middle
    return jnp.concatenate([high, middle, low], axis=0).astype(jnp.bfloat16)


def select(value, onehot):
    rows = value.shape[0]
    product = lax.dot_general(split3(value), onehot, (((1,), (0,)), ((), ())), preferred_element_type=jnp.float32)
    return product[:rows] + product[rows : 2 * rows] + product[2 * rows :]


def spread_select(value, onehot):
    rows = value.shape[0]
    product = lax.dot_general(
        split3(value), onehot, (((1, 2), (1, 2)), ((), ())), preferred_element_type=jnp.float32
    )
    return product[:rows] + product[rows : 2 * rows] + product[2 * rows :]


def chip_sum(value, axis):
    count = lax.axis_size(axis)
    if count != 4:
        return jnp.sum(lax.all_gather(value, axis), axis=0)
    from_next = ring(value, axis, -1)
    from_prev = ring(value, axis, 1)
    opposite = ring(from_next, axis, -1)
    relative = jnp.stack([value, from_next, opposite, from_prev])
    ordered = jnp.roll(relative, lax.axis_index(axis), axis=0)
    return jnp.sum(ordered, axis=0)


def ring(value, axis, step):
    count = lax.axis_size(axis)
    return lax.ppermute(value, axis, [(i, (i + step) % count) for i in range(count)])


def on_device(
    latent,
    stencil,
    bin_width,
    neighbours,
    star_bin,
    star_pixels,
    star_weights,
    star_frac,
    observed,
    sigma,
):
    shells, pixels = latent.shape
    taps = neighbours.shape[0]
    frame = pixels + 2 * COLS

    before = ring(latent, "ang", 1)
    after = ring(latent, "ang", -1)
    wide = jnp.concatenate([before[:, pixels - COLS :], latent, after[:, :COLS]], axis=1)

    position = lax.broadcasted_iota(jnp.int32, (frame, taps, pixels), 0)
    pick = (position == neighbours[None, :, :]).astype(jnp.bfloat16)
    picked = select(wide, pick)
    refined = jnp.sum(picked * stencil[:, :, None], axis=1)
    density = jnp.exp(refined)
    weighted = bin_width[:, None] * density

    nstars = star_bin.shape[0]
    pixel_id = lax.broadcasted_iota(jnp.int32, (pixels, nstars), 0)
    spread = jnp.sum(jnp.where(pixel_id[None] == star_pixels[:, None, :], star_weights[:, None, :], 0.0), axis=0)

    shell_start = (lax.axis_index("zhi") * lax.axis_size("core") + lax.axis_index("core")) * shells
    bin_id = shell_start + lax.broadcasted_iota(jnp.int32, (shells, nstars), 0)
    lower = star_bin[None, :]
    radial = jnp.where(bin_id <= lower, 1.0, jnp.where(bin_id - 1 == lower, star_frac[None, :], 0.0))

    at_stars = jnp.dot(weighted, spread, precision=HIGHEST, preferred_element_type=jnp.float32)
    partial_value = jnp.sum(radial * at_stars, axis=0)
    predicted = lax.psum(chip_sum(partial_value, "zhi"), "core")
    weight_back = (predicted - observed) / (sigma * sigma)

    adjoint_sum = lax.dot_general(
        radial * weight_back[None, :],
        spread,
        (((1,), (1,)), ((), ())),
        precision=HIGHEST,
        preferred_element_type=jnp.float32,
    )
    sensitivity = adjoint_sum * weighted

    terms = stencil[:, :, None] * sensitivity[:, None, :]
    edge_id = lax.broadcasted_iota(jnp.int32, (2 * COLS, taps, pixels), 0)
    edge_id = edge_id + jnp.where(edge_id >= COLS, frame - 2 * COLS, 0)
    edges = spread_select(terms, (edge_id == neighbours[None]).astype(jnp.bfloat16))
    to_after, to_before = lax.optimization_barrier((edges[:, COLS:], edges[:, :COLS]))
    from_before = ring(to_after, "ang", 1)
    from_after = ring(to_before, "ang", -1)
    own_id = COLS + lax.broadcasted_iota(jnp.int32, (pixels, taps, pixels), 0)
    inner = spread_select(terms, (own_id == neighbours[None]).astype(jnp.bfloat16))
    gradient = inner + jnp.pad(from_before, ((0, 0), (0, pixels - COLS))) + jnp.pad(
        from_after, ((0, 0), (pixels - COLS, 0))
    )
    return (predicted, gradient)


def solution(mesh):
    ang, rad = mesh.devices.shape
    split = Mesh(mesh.devices.reshape(ang, rad // 2, 2), ("ang", "zhi", "core"))
    shell = ("zhi", "core")
    return jax.shard_map(
        on_device,
        mesh=split,
        in_specs=(
            P(shell, "ang"),
            P(shell, None),
            P(shell),
            P(None, "ang"),
            P("ang"),
            P(None, "ang"),
            P(None, "ang"),
            P("ang"),
            P("ang"),
            P("ang"),
        ),
        out_specs=(P("ang"), P(shell, "ang")),
        check_vma=False,
    )
```
